32 devices in a mesh: lon: 8 (over z, y), lat: 4 (over x, core).
Axes of the slice: x: 2, y: 2, z: 4, core: 2. Of those that a mesh axis runs over, the one named last changes fastest.
Arguments:
- potential_warmth: float32 [25, 64, 2048], P(None, 'lat', 'lon'), may hold values from -6 to 6
- saltiness_anomaly: float32 [25, 64, 2048], P(None, 'lat', 'lon'), may hold values from -6 to 6
- zonal_speed: float32 [25, 64, 2048], P(None, 'lat', 'lon'), may hold values from -0.625 to 0.625
- meridional_speed: float32 [25, 64, 2048], P(None, 'lat', 'lon'), may hold values from -0.625 to 0.625
- sinking_speed: float32 [25, 64, 2048], P(None, 'lat', 'lon'), may hold values from -0.625 to 0.625
- water_indicator: int32 [64, 2048], P('lat', 'lon'), may hold values from 0 to 1, as said below
- seabed_layer_index: int32 [64, 2048], P('lat', 'lon'), may hold values from 1 to 25
Outputs:
- new_temperature: float32 [25, 64, 2048], P(None, 'lat', 'lon')
- new_salinity: float32 [25, 64, 2048], P(None, 'lat', 'lon')
The draws below stay inside these ranges and needn't reach their ends.
Inputs may be any that keep to these rules, and one draw needn't show every extreme that they name: `water_indicator`: 1 marks a sea column, 0 a land column. `seabed_layer_index`: levels of a column counted from the top.
All inputs are finite; a program needn't handle non-finite values.
Results may differ from the reference program's by a relative error of at most 0.0003.
Values sent between devices are 32-bit elements; how exact they have to be, the bound alone decides.
No kernel may reach another device: no remote copies, remote signals or barrier semaphores. Data moves between devices by JAX's collectives and lax.ppermute only.
A program may use at most 64 MiB of HBM per device.

```python
import jax
import jax.numpy as jnp
from jax import lax

CX = 256
CY = 16
STRATA_NUMBER = 25
PARALLEL_POINTS = 2048
MERIDIAN_POINTS = 64


def draw_water_indicator(key, part):
    tile_key, cell_key = jax.random.split(jax.random.fold_in(key, 17))
    tile_rows = MERIDIAN_POINTS // CY
    tile_cols = PARALLEL_POINTS // CX
    land_level = jax.random.randint(tile_key, (tile_rows, tile_cols), 0, 5)
    spread = jnp.repeat(jnp.repeat(land_level, CY, axis=0), CX, axis=1)
    cell_level = jax.random.randint(cell_key, (MERIDIAN_POINTS, PARALLEL_POINTS), 0, 4)
    return jnp.where(cell_level >= spread, 1, 0).astype(jnp.int32)


def plant(entries, stream_key, least, largest):
    dims = entries.shape
    index_at = [jax.random.randint(jax.random.fold_in(stream_key, axis), (), 0, dims[axis]) for axis in range(len(dims))]
    entries = entries.at[tuple(index_at)].set(least)
    longest = dims.index(max(dims))
    index_at[longest] = (index_at[longest] + 1) % dims[longest]
    return entries.at[tuple(index_at)].set(largest)


def shard_levels(key, dims, shards, least, largest):
    factor_of, own = 1.0, jax.random.fold_in(key, 6)
    for dim, shards_of in shards:
        steps = jnp.exp(jax.random.uniform(jax.random.fold_in(own, dim), (shards_of,), jnp.float32, least / len(shards), largest / len(shards)))
        factor_of = factor_of * jnp.repeat(steps, dims[dim] // shards_of).reshape([-1 if axis == dim else 1 for axis in range(len(dims))])
    return factor_of


def scatter_about(stream_key, dims, deviation, limit, shards=(), kind=jnp.bfloat16):
    entries = jax.random.normal(stream_key, dims, jnp.float32) * deviation
    if len(shards) > 0:
        entries = shard_levels(stream_key, dims, shards, -0.22, 0.18) * entries
    return jnp.clip(entries, min=-limit, max=limit).astype(kind)


def setup_inputs(seed: int = 0) -> dict:
    streams_of = jax.random.split(jax.random.key(seed), 8)
    return {
        "potential_warmth": scatter_about(streams_of[0], (STRATA_NUMBER, MERIDIAN_POINTS, PARALLEL_POINTS), 1.0, 6.0, ((1, 4), (2, 8)), jnp.float32),
        "saltiness_anomaly": scatter_about(streams_of[1], (STRATA_NUMBER, MERIDIAN_POINTS, PARALLEL_POINTS), 1.0, 6.0, ((1, 4), (2, 8)), jnp.float32),
        "zonal_speed": scatter_about(streams_of[2], (STRATA_NUMBER, MERIDIAN_POINTS, PARALLEL_POINTS), 0.1, 0.625, ((1, 4), (2, 8)), jnp.float32),
        "meridional_speed": scatter_about(streams_of[3], (STRATA_NUMBER, MERIDIAN_POINTS, PARALLEL_POINTS), 0.1, 0.625, ((1, 4), (2, 8)), jnp.float32),
        "sinking_speed": scatter_about(streams_of[4], (STRATA_NUMBER, MERIDIAN_POINTS, PARALLEL_POINTS), 0.1, 0.625, ((1, 4), (2, 8)), jnp.float32),
        "water_indicator": draw_water_indicator(jax.random.fold_in(streams_of[7], 71), 0),
        "seabed_layer_index": plant(jax.random.randint(streams_of[6], (MERIDIAN_POINTS, PARALLEL_POINTS), 1, STRATA_NUMBER + 1), jax.random.fold_in(streams_of[6], 1), 1, STRATA_NUMBER).astype(jnp.int32),
    }


DIFFUSIVITY = 0.15
DENSITY_FLOOR = 0.5
SLOPE_LIMIT = 1.0
THERMAL = 0.25
HALINE = 0.75


def tracer_step(extended, sinking_speed):
    layer_total = sinking_speed.shape[0]
    temp_ext = extended[:layer_total]
    salt_ext = extended[layer_total:2 * layer_total]
    depth_ext = extended[2 * layer_total]
    east_ext = extended[2 * layer_total + 1:3 * layer_total + 1]
    north_ext = extended[3 * layer_total + 1:]
    level_index = jnp.arange(layer_total).astype(depth_ext.dtype)[:, None, None]
    wet_cells = jnp.where(level_index < depth_ext[None], 1.0, 0.0).astype(depth_ext.dtype)
    east_face = wet_cells[:, 1:-1, :-1] * wet_cells[:, 1:-1, 1:]
    north_face = wet_cells[:, :-1, 1:-1] * wet_cells[:, 1:, 1:-1]
    upper_full = wet_cells[1:] * wet_cells[:-1]
    upper_face = upper_full[:, 1:-1, 1:-1]

    def gradients(values):
        grad_east = (values[:, 1:-1, 1:] - values[:, 1:-1, :-1]) * east_face
        grad_north = (values[:, 1:, 1:-1] - values[:, :-1, 1:-1]) * north_face
        grad_down = (values[1:] - values[:-1]) * upper_full
        zero_plane = jnp.zeros_like(grad_down[:1])
        vert_cell = 0.5 * (jnp.concatenate([zero_plane, grad_down], 0) + jnp.concatenate([grad_down, zero_plane], 0))
        vert_east = 0.5 * (vert_cell[:, 1:-1, :-1] + vert_cell[:, 1:-1, 1:])
        vert_north = 0.5 * (vert_cell[:, :-1, 1:-1] + vert_cell[:, 1:, 1:-1])
        east_cell = 0.5 * (grad_east[:, :, :-1] + grad_east[:, :, 1:])
        north_cell = 0.5 * (grad_north[:, :-1] + grad_north[:, 1:])
        east_upper = 0.5 * (east_cell[:-1] + east_cell[1:])
        north_upper = 0.5 * (north_cell[:-1] + north_cell[1:])
        return grad_east, grad_north, grad_down[:, 1:-1, 1:-1], vert_east, vert_north, east_upper, north_upper

    density = HALINE * salt_ext - THERMAL * temp_ext
    rho_east, rho_north, rho_down, rho_vert_east, rho_vert_north, rho_east_upper, rho_north_upper = gradients(density)
    slope_east = jnp.clip(-rho_east / jnp.maximum(rho_vert_east, DENSITY_FLOOR), -SLOPE_LIMIT, SLOPE_LIMIT)
    slope_north = jnp.clip(-rho_north / jnp.maximum(rho_vert_north, DENSITY_FLOOR), -SLOPE_LIMIT, SLOPE_LIMIT)
    slope_x = jnp.clip(-rho_east_upper / jnp.maximum(rho_down, DENSITY_FLOOR), -SLOPE_LIMIT, SLOPE_LIMIT)
    slope_y = jnp.clip(-rho_north_upper / jnp.maximum(rho_down, DENSITY_FLOOR), -SLOPE_LIMIT, SLOPE_LIMIT)
    flow_east = 0.5 * (east_ext[:, 1:-1, :-1] + east_ext[:, 1:-1, 1:]) * east_face
    flow_north = 0.5 * (north_ext[:, :-1, 1:-1] + north_ext[:, 1:, 1:-1]) * north_face
    flow_down = 0.5 * (sinking_speed[:-1] + sinking_speed[1:]) * upper_face

    def advance(values):
        grad_east, grad_north, grad_down, vert_east, vert_north, east_upper, north_upper = gradients(values)
        own_cells = values[:, 1:-1, 1:-1]
        flux_east = (jnp.maximum(flow_east, 0.0) * values[:, 1:-1, :-1] + jnp.minimum(flow_east, 0.0) * values[:, 1:-1, 1:]
                     - DIFFUSIVITY * east_face * (grad_east + slope_east * vert_east))
        flux_north = (jnp.maximum(flow_north, 0.0) * values[:, :-1, 1:-1] + jnp.minimum(flow_north, 0.0) * values[:, 1:, 1:-1]
                      - DIFFUSIVITY * north_face * (grad_north + slope_north * vert_north))
        flux_down = (jnp.maximum(flow_down, 0.0) * own_cells[:-1] + jnp.minimum(flow_down, 0.0) * own_cells[1:]
                     - DIFFUSIVITY * upper_face * (slope_x * east_upper + slope_y * north_upper
                                                   + (slope_x * slope_x + slope_y * slope_y) * grad_down))
        zero_plane = jnp.zeros_like(flux_down[:1])
        divergence = (flux_east[:, :, 1:] - flux_east[:, :, :-1]) + (flux_north[:, 1:] - flux_north[:, :-1])
        divergence = divergence + (jnp.concatenate([flux_down, zero_plane], 0) - jnp.concatenate([zero_plane, flux_down], 0))
        return own_cells - divergence

    return advance(temp_ext), advance(salt_ext)


def reference(potential_warmth, saltiness_anomaly, zonal_speed, meridional_speed, sinking_speed, water_indicator, seabed_layer_index):
    layer_total = potential_warmth.shape[0]
    strata_total = (water_indicator * seabed_layer_index).astype(potential_warmth.dtype)[None]
    joined_scalar_fields = jnp.concatenate([potential_warmth, saltiness_anomaly, strata_total, zonal_speed, meridional_speed], 0)
    wrapped = jnp.concatenate([joined_scalar_fields[:, :, -1:], joined_scalar_fields, joined_scalar_fields[:, :, :1]], 2)
    base_planes = 2 * layer_total + 1
    top_line = joined_scalar_fields[:, -1, ::-1]
    fold_line = jnp.concatenate([top_line[:base_planes],
                                 jnp.zeros_like(top_line[base_planes:base_planes + layer_total]),
                                 -top_line[base_planes + layer_total:]], 0)
    north_line = jnp.pad(fold_line, ((0, 0), (1, 1)))[:, None]
    south_line = jnp.zeros_like(north_line)
    extended = jnp.concatenate([south_line, wrapped, north_line], 1)
    block_count = MERIDIAN_POINTS // CY

    def one_block(block_index):
        start = (block_index * CY).astype(jnp.int32)
        rows_ext = lax.dynamic_slice_in_dim(extended, start, CY + 2, 1)
        down_rows = lax.dynamic_slice_in_dim(sinking_speed, start, CY, 1)
        return tracer_step(rows_ext, down_rows)

    new_temp, new_salt = lax.map(one_block, jnp.arange(block_count, dtype=jnp.int32))
    new_temp = jnp.transpose(new_temp, (1, 0, 2, 3)).reshape(layer_total, MERIDIAN_POINTS, PARALLEL_POINTS)
    new_salt = jnp.transpose(new_salt, (1, 0, 2, 3)).reshape(layer_total, MERIDIAN_POINTS, PARALLEL_POINTS)
    return new_temp, new_salt
```

```python
import jax
import jax.numpy as jnp
from jax import lax
from jax.sharding import PartitionSpec as P

DIFFUSIVITY = 0.15
DENSITY_FLOOR = 0.5
SLOPE_LIMIT = 1.0
THERMAL = 0.25
HALINE = 0.75


def extended_2(cells, sides, width, closed):
    for axis, dim in sides:
        count = lax.axis_size(axis)
        ends = count if closed else count - 1
        head = lax.slice_in_dim(cells, 0, width, axis=dim)
        tail = lax.slice_in_dim(cells, cells.shape[dim] - width, cells.shape[dim], axis=dim)
        cells = jnp.concatenate(
            [
                lax.ppermute(tail, axis, [(i, (i + 1) % count) for i in range(ends)]),
                cells,
                lax.ppermute(head, axis, [((i + 1) % count, i) for i in range(ends)]),
            ],
            axis=dim,
        )
    return cells


def tracer_step(extended, sinking_speed):
    layer_total = sinking_speed.shape[0]
    temp_ext = extended[:layer_total]
    salt_ext = extended[layer_total : 2 * layer_total]
    depth_ext = extended[2 * layer_total]
    east_ext = extended[2 * layer_total + 1 : 3 * layer_total + 1]
    north_ext = extended[3 * layer_total + 1 :]
    level_index = jnp.arange(layer_total).astype(depth_ext.dtype)[:, None, None]
    wet_cells = jnp.where(level_index < depth_ext[None], 1.0, 0.0).astype(depth_ext.dtype)
    east_face = wet_cells[:, 1:-1, :-1] * wet_cells[:, 1:-1, 1:]
    north_face = wet_cells[:, :-1, 1:-1] * wet_cells[:, 1:, 1:-1]
    upper_full = wet_cells[1:] * wet_cells[:-1]
    upper_face = upper_full[:, 1:-1, 1:-1]

    def gradients(values):
        grad_east = (values[:, 1:-1, 1:] - values[:, 1:-1, :-1]) * east_face
        grad_north = (values[:, 1:, 1:-1] - values[:, :-1, 1:-1]) * north_face
        grad_down = (values[1:] - values[:-1]) * upper_full
        zero_plane = jnp.zeros_like(grad_down[:1])
        vert_cell = 0.5 * (
            jnp.concatenate([zero_plane, grad_down], 0)
            + jnp.concatenate([grad_down, zero_plane], 0)
        )
        vert_east = 0.5 * (vert_cell[:, 1:-1, :-1] + vert_cell[:, 1:-1, 1:])
        vert_north = 0.5 * (vert_cell[:, :-1, 1:-1] + vert_cell[:, 1:, 1:-1])
        east_cell = 0.5 * (grad_east[:, :, :-1] + grad_east[:, :, 1:])
        north_cell = 0.5 * (grad_north[:, :-1] + grad_north[:, 1:])
        east_upper = 0.5 * (east_cell[:-1] + east_cell[1:])
        north_upper = 0.5 * (north_cell[:-1] + north_cell[1:])
        return (
            grad_east,
            grad_north,
            grad_down[:, 1:-1, 1:-1],
            vert_east,
            vert_north,
            east_upper,
            north_upper,
        )

    density = HALINE * salt_ext - THERMAL * temp_ext
    (
        rho_east,
        rho_north,
        rho_down,
        rho_vert_east,
        rho_vert_north,
        rho_east_upper,
        rho_north_upper,
    ) = gradients(density)
    slope_east = jnp.clip(
        -rho_east / jnp.maximum(rho_vert_east, DENSITY_FLOOR), -SLOPE_LIMIT, SLOPE_LIMIT
    )
    slope_north = jnp.clip(
        -rho_north / jnp.maximum(rho_vert_north, DENSITY_FLOOR), -SLOPE_LIMIT, SLOPE_LIMIT
    )
    slope_x = jnp.clip(
        -rho_east_upper / jnp.maximum(rho_down, DENSITY_FLOOR), -SLOPE_LIMIT, SLOPE_LIMIT
    )
    slope_y = jnp.clip(
        -rho_north_upper / jnp.maximum(rho_down, DENSITY_FLOOR), -SLOPE_LIMIT, SLOPE_LIMIT
    )
    flow_east = 0.5 * (east_ext[:, 1:-1, :-1] + east_ext[:, 1:-1, 1:]) * east_face
    flow_north = 0.5 * (north_ext[:, :-1, 1:-1] + north_ext[:, 1:, 1:-1]) * north_face
    flow_down = 0.5 * (sinking_speed[:-1] + sinking_speed[1:]) * upper_face

    def advance(values):
        grad_east, grad_north, grad_down, vert_east, vert_north, east_upper, north_upper = (
            gradients(values)
        )
        own_cells = values[:, 1:-1, 1:-1]
        flux_east = (
            jnp.maximum(flow_east, 0.0) * values[:, 1:-1, :-1]
            + jnp.minimum(flow_east, 0.0) * values[:, 1:-1, 1:]
            - DIFFUSIVITY * east_face * (grad_east + slope_east * vert_east)
        )
        flux_north = (
            jnp.maximum(flow_north, 0.0) * values[:, :-1, 1:-1]
            + jnp.minimum(flow_north, 0.0) * values[:, 1:, 1:-1]
            - DIFFUSIVITY * north_face * (grad_north + slope_north * vert_north)
        )
        flux_down = (
            jnp.maximum(flow_down, 0.0) * own_cells[:-1]
            + jnp.minimum(flow_down, 0.0) * own_cells[1:]
            - DIFFUSIVITY
            * upper_face
            * (
                slope_x * east_upper
                + slope_y * north_upper
                + (slope_x * slope_x + slope_y * slope_y) * grad_down
            )
        )
        zero_plane = jnp.zeros_like(flux_down[:1])
        divergence = (
            flux_east[:, :, 1:] - flux_east[:, :, :-1] + (flux_north[:, 1:] - flux_north[:, :-1])
        )
        divergence = divergence + (
            jnp.concatenate([flux_down, zero_plane], 0)
            - jnp.concatenate([zero_plane, flux_down], 0)
        )
        return own_cells - divergence

    return (advance(temp_ext), advance(salt_ext))


def framed(centre, west_cols, east_cols, south_rows, north_rows):
    middle = jnp.concatenate([west_cols, centre, east_cols], 2)
    lower_rows = jnp.pad(south_rows, ((0, 0), (0, 0), (1, 1)))
    upper_rows = jnp.pad(north_rows, ((0, 0), (0, 0), (1, 1)))
    return jnp.concatenate([lower_rows, middle, upper_rows], 1)


def on_device(
    potential_warmth,
    saltiness_anomaly,
    zonal_speed,
    meridional_speed,
    sinking_speed,
    water_indicator,
    seabed_layer_index,
):
    layer_total = potential_warmth.shape[0]
    base_planes = 2 * layer_total + 1
    strata_total = (water_indicator * seabed_layer_index).astype(jnp.float32)[None]
    scalar_field_strata = jnp.concatenate([potential_warmth, saltiness_anomaly, strata_total], 0)
    lon_count = lax.axis_size("lon")
    lat_count = lax.axis_size("lat")
    top_row = lax.axis_index("lat") == lat_count - 1
    lon_fields = jnp.concatenate([scalar_field_strata, zonal_speed], 0)
    west_cols = lax.ppermute(
        lon_fields[:, :, -1:], "lon", [(i, (i + 1) % lon_count) for i in range(lon_count)]
    )
    east_cols = lax.ppermute(
        lon_fields[:, :, :1], "lon", [((i + 1) % lon_count, i) for i in range(lon_count)]
    )
    lat_fields = jnp.concatenate([scalar_field_strata, meridional_speed], 0)
    south_rows = lax.ppermute(
        lat_fields[:, -1:, :], "lat", [(i, i + 1) for i in range(lat_count - 1)]
    )
    north_rows = lax.ppermute(
        lat_fields[:, :1, :], "lat", [(i + 1, i) for i in range(lat_count - 1)]
    )
    facing = lax.ppermute(
        lat_fields[:, -1:, :], "lon", [(i, lon_count - 1 - i) for i in range(lon_count)]
    )[:, :, ::-1]
    ghost_row = jnp.concatenate([facing[:base_planes], -facing[base_planes:]], 0)
    north_rows = jnp.where(top_row, ghost_row, north_rows)
    col_zeros = jnp.zeros((layer_total,) + west_cols.shape[1:], jnp.float32)
    row_zeros = jnp.zeros((layer_total,) + south_rows.shape[1:], jnp.float32)
    west_cols = jnp.concatenate([west_cols, col_zeros], 0)
    east_cols = jnp.concatenate([east_cols, col_zeros], 0)
    south_rows = jnp.concatenate([south_rows[:base_planes], row_zeros, south_rows[base_planes:]], 0)
    north_rows = jnp.concatenate([north_rows[:base_planes], row_zeros, north_rows[base_planes:]], 0)
    centre = jnp.concatenate([scalar_field_strata, zonal_speed, meridional_speed], 0)
    extended = framed(centre, west_cols, east_cols, south_rows, north_rows)
    return tracer_step(extended, sinking_speed)


def solution(mesh):
    placed = (
        P(None, "lat", "lon"),
        P(None, "lat", "lon"),
        P(None, "lat", "lon"),
        P(None, "lat", "lon"),
        P(None, "lat", "lon"),
        P("lat", "lon"),
        P("lat", "lon"),
    )
    return jax.shard_map(
        on_device,
        mesh=mesh,
        in_specs=placed,
        out_specs=(P(None, "lat", "lon"), P(None, "lat", "lon")),
        check_vma=False,
    )
```

```python
import jax
import jax.numpy as jnp
from jax import lax
from jax.experimental import pallas as pl
from jax.experimental.pallas import tpu as pltpu
from jax.sharding import PartitionSpec as P

DIFFUSIVITY = 0.15
DENSITY_FLOOR = 0.5
SLOPE_LIMIT = 1.0
THERMAL = 0.25
HALINE = 0.75


def stencil_kernel(
    t_ref, s_ref, u_ref, v_ref, w_ref, d_ref, hw_ref, he_ref, hs_ref, hn_ref,
    ot_ref, os_ref, tsh, ssh, ush, vsh, dsh,
):
    layer_total, rows, cols = t_ref.shape
    lane = lax.broadcasted_iota(jnp.int32, (rows, cols), 1)
    row = lax.broadcasted_iota(jnp.int32, (rows, cols), 0)
    east_edge = lane == cols - 1
    west_edge = lane == 0
    north_edge = row == rows - 1
    south_edge = row == 0

    def east_of(x, h):
        return jnp.where(east_edge, h, pltpu.roll(x, cols - 1, 1))

    def west_of(x, h):
        return jnp.where(west_edge, h, pltpu.roll(x, 1, 1))

    def north_of(x, h):
        return jnp.where(north_edge, h, pltpu.roll(x, rows - 1, 0))

    def south_of(x, h):
        return jnp.where(south_edge, h, pltpu.roll(x, 1, 0))

    depth_plane = 2 * layer_total
    depth = d_ref[...]
    dsh[0] = depth
    dsh[1] = east_of(depth, he_ref[depth_plane])
    dsh[2] = west_of(depth, hw_ref[depth_plane])
    dsh[3] = north_of(depth, hn_ref[depth_plane])
    dsh[4] = south_of(depth, hs_ref[depth_plane])

    def prepare(k, carry):
        for src, dst, base in ((t_ref, tsh, 0), (s_ref, ssh, layer_total)):
            x = src[k]
            dst[0, k] = east_of(x, he_ref[base + k])
            dst[1, k] = west_of(x, hw_ref[base + k])
            dst[2, k] = north_of(x, hn_ref[base + k])
            dst[3, k] = south_of(x, hs_ref[base + k])
        x = u_ref[k]
        ush[0, k] = east_of(x, he_ref[depth_plane + 1 + k])
        ush[1, k] = west_of(x, hw_ref[depth_plane + 1 + k])
        x = v_ref[k]
        vsh[0, k] = north_of(x, hn_ref[depth_plane + 1 + k])
        vsh[1, k] = south_of(x, hs_ref[depth_plane + 1 + k])
        return carry

    lax.fori_loop(0, layer_total, prepare, 0)

    def planes(k):
        at = jnp.clip(k, 0, layer_total - 1)
        temp = [t_ref[at]] + [tsh[i, at] for i in range(4)]
        salt = [s_ref[at]] + [ssh[i, at] for i in range(4)]
        rho = [HALINE * sv - THERMAL * tv for tv, sv in zip(temp, salt)]
        return temp, salt, rho

    def wet_at(k):
        inside = jnp.logical_and(k >= 0, k < layer_total)
        level = k.astype(jnp.float32)
        return [
            jnp.where(jnp.logical_and(inside, level < dsh[i]), 1.0, 0.0) for i in range(5)
        ]

    def horizontal(fields, kcs, wet, a, b, speed_a, speed_b, slope_of):
        face = wet[a] * wet[b]
        temp, salt, rho = fields
        k_temp, k_salt, k_rho = kcs
        slope = jnp.clip(
            -((rho[b] - rho[a]) * face)
            / jnp.maximum(0.5 * (k_rho[a] + k_rho[b]), DENSITY_FLOOR),
            -SLOPE_LIMIT,
            SLOPE_LIMIT,
        )
        flow = 0.5 * (speed_a + speed_b) * face
        up, down = jnp.maximum(flow, 0.0), jnp.minimum(flow, 0.0)
        out = []
        for x, kx in ((temp, k_temp), (salt, k_salt)):
            grad = (x[b] - x[a]) * face
            out.append(
                up * x[a] + down * x[b]
                - DIFFUSIVITY * face * (grad + slope * (0.5 * (kx[a] + kx[b])))
            )
        return out

    def cell_means(x, wet):
        east_grad = (x[1] - x[0]) * (wet[0] * wet[1])
        west_grad = (x[0] - x[2]) * (wet[2] * wet[0])
        north_grad = (x[3] - x[0]) * (wet[0] * wet[3])
        south_grad = (x[0] - x[4]) * (wet[4] * wet[0])
        return 0.5 * (west_grad + east_grad), 0.5 * (south_grad + north_grad)

    def level_step(k, carry):
        down_temp, down_salt = carry
        lower = planes(k - 1)
        here = planes(k)
        upper = planes(k + 1)
        wet_lower = wet_at(k - 1)
        wet_here = wet_at(k)
        wet_upper = wet_at(k + 1)
        face_top = [wet_here[i] * wet_lower[i] for i in range(5)]
        face_bottom = [wet_upper[i] * wet_here[i] for i in range(5)]
        kcs = [
            [
                0.5 * ((h[i] - lo[i]) * face_top[i] + (up[i] - h[i]) * face_bottom[i])
                for i in range(5)
            ]
            for lo, h, up in zip(lower, here, upper)
        ]
        zonal = u_ref[k]
        meridional = v_ref[k]
        east = horizontal(here, kcs, wet_here, 0, 1, zonal, ush[0, k], None)
        west = horizontal(here, kcs, wet_here, 2, 0, ush[1, k], zonal, None)
        north = horizontal(here, kcs, wet_here, 0, 3, meridional, vsh[0, k], None)
        south = horizontal(here, kcs, wet_here, 4, 0, vsh[1, k], meridional, None)
        means_here = [cell_means(f, wet_here) for f in here]
        means_upper = [cell_means(f, wet_upper) for f in upper]
        face = face_bottom[0]
        xu = [0.5 * (mh[0] + mu[0]) for mh, mu in zip(means_here, means_upper)]
        yu = [0.5 * (mh[1] + mu[1]) for mh, mu in zip(means_here, means_upper)]
        dk = [(up[0] - h[0]) * face for h, up in zip(here, upper)]
        floor = jnp.maximum(dk[2], DENSITY_FLOOR)
        slope_x = jnp.clip(-xu[2] / floor, -SLOPE_LIMIT, SLOPE_LIMIT)
        slope_y = jnp.clip(-yu[2] / floor, -SLOPE_LIMIT, SLOPE_LIMIT)
        above = jnp.clip(k + 1, 0, layer_total - 1)
        flow = 0.5 * (w_ref[k] + w_ref[above]) * face
        up, down = jnp.maximum(flow, 0.0), jnp.minimum(flow, 0.0)
        squares = slope_x * slope_x + slope_y * slope_y
        below = []
        for n in range(2):
            below.append(
                up * here[n][0] + down * upper[n][0]
                - DIFFUSIVITY * face * (slope_x * xu[n] + slope_y * yu[n] + squares * dk[n])
            )
        for n, (dst, top) in enumerate(((ot_ref, down_temp), (os_ref, down_salt))):
            divergence = (east[n] - west[n]) + (north[n] - south[n])
            divergence = divergence + (below[n] - top)
            dst[k] = here[n][0] - divergence
        return tuple(below)

    zero = jnp.zeros((rows, cols), jnp.float32)
    lax.fori_loop(0, layer_total, level_step, (zero, zero))


def on_device(
    potential_warmth,
    saltiness_anomaly,
    zonal_speed,
    meridional_speed,
    sinking_speed,
    water_indicator,
    seabed_layer_index,
):
    layer_total, rows, cols = potential_warmth.shape
    base_planes = 2 * layer_total + 1
    depth = (water_indicator * seabed_layer_index).astype(jnp.float32)
    lon_count = lax.axis_size("lon")
    lat_count = lax.axis_size("lat")
    top_row = lax.axis_index("lat") == lat_count - 1

    def column(at):
        return jnp.concatenate(
            [
                potential_warmth[:, :, at],
                saltiness_anomaly[:, :, at],
                depth[None, :, at],
                zonal_speed[:, :, at],
            ],
            0,
        )[:, :, None]

    def line(at):
        return jnp.concatenate(
            [
                potential_warmth[:, at],
                saltiness_anomaly[:, at],
                depth[None, at],
                meridional_speed[:, at],
            ],
            0,
        )[:, None]

    west_cols = lax.ppermute(
        column(cols - 1), "lon", [(i, (i + 1) % lon_count) for i in range(lon_count)]
    )
    east_cols = lax.ppermute(
        column(0), "lon", [((i + 1) % lon_count, i) for i in range(lon_count)]
    )
    top_line = line(rows - 1)
    south_rows = lax.ppermute(top_line, "lat", [(i, i + 1) for i in range(lat_count - 1)])
    north_rows = lax.ppermute(line(0), "lat", [(i + 1, i) for i in range(lat_count - 1)])
    facing = lax.ppermute(
        top_line, "lon", [(i, lon_count - 1 - i) for i in range(lon_count)]
    )[:, :, ::-1]
    ghost_row = jnp.concatenate([facing[:base_planes], -facing[base_planes:]], 0)
    north_rows = jnp.where(top_row, ghost_row, north_rows)

    field = jax.ShapeDtypeStruct(potential_warmth.shape, jnp.float32)
    vmem = pltpu.MemorySpace.VMEM
    return pl.pallas_call(
        stencil_kernel,
        out_shape=(field, field),
        in_specs=[pl.BlockSpec(memory_space=vmem)] * 10,
        out_specs=(pl.BlockSpec(memory_space=vmem), pl.BlockSpec(memory_space=vmem)),
        scratch_shapes=[
            pltpu.VMEM((4, layer_total, rows, cols), jnp.float32),
            pltpu.VMEM((4, layer_total, rows, cols), jnp.float32),
            pltpu.VMEM((2, layer_total, rows, cols), jnp.float32),
            pltpu.VMEM((2, layer_total, rows, cols), jnp.float32),
            pltpu.VMEM((5, rows, cols), jnp.float32),
        ],
    )(
        potential_warmth,
        saltiness_anomaly,
        zonal_speed,
        meridional_speed,
        sinking_speed,
        depth,
        west_cols,
        east_cols,
        south_rows,
        north_rows,
    )


def solution(mesh):
    placed = (
        P(None, "lat", "lon"),
        P(None, "lat", "lon"),
        P(None, "lat", "lon"),
        P(None, "lat", "lon"),
        P(None, "lat", "lon"),
        P("lat", "lon"),
        P("lat", "lon"),
    )
    return jax.shard_map(
        on_device,
        mesh=mesh,
        in_specs=placed,
        out_specs=(P(None, "lat", "lon"), P(None, "lat", "lon")),
        check_vma=False,
    )
```

```python
import jax
import jax.numpy as jnp
from jax import lax
from jax.experimental import pallas as pl
from jax.experimental.pallas import tpu as pltpu
from jax.sharding import PartitionSpec as P

DIFFUSIVITY = 0.15
DENSITY_FLOOR = 0.5
SLOPE_LIMIT = 1.0
THERMAL = 0.25
HALINE = 0.75


def stencil_kernel(
    t_ref, s_ref, u_ref, v_ref, w_ref, d_ref, hw_ref, he_ref, hs_ref, hn_ref,
    ot_ref, os_ref, tsh, ssh, ush, vsh, dsh,
):
    layer_total, rows, cols = t_ref.shape
    lane = lax.broadcasted_iota(jnp.int32, (rows, cols), 1)
    row = lax.broadcasted_iota(jnp.int32, (rows, cols), 0)
    east_edge = lane == cols - 1
    west_edge = lane == 0
    north_edge = row == rows - 1
    south_edge = row == 0

    def east_of(x, h):
        return jnp.where(east_edge, h, pltpu.roll(x, cols - 1, 1))

    def west_of(x, h):
        return jnp.where(west_edge, h, pltpu.roll(x, 1, 1))

    def north_of(x, h):
        return jnp.where(north_edge, h, pltpu.roll(x, rows - 1, 0))

    def south_of(x, h):
        return jnp.where(south_edge, h, pltpu.roll(x, 1, 0))

    lane_tile = hw_ref.shape[1]

    def column_of(ref, p, at):
        packed = ref[...]
        shift = (at - p) % lane_tile
        if shift:
            packed = pltpu.roll(packed, shift, 1)
        return jnp.concatenate([packed] * (cols // lane_tile), 1)

    def east_halo(p):
        return column_of(he_ref, p, lane_tile - 1)

    def west_halo(p):
        return column_of(hw_ref, p, 0)

    def north_halo(p):
        return hn_ref[p : p + 1, :]

    def south_halo(p):
        return hs_ref[p : p + 1, :]

    depth_plane = 2 * layer_total
    depth = (d_ref[0] * d_ref[1]).astype(jnp.float32)
    dsh[0] = depth
    dsh[1] = east_of(depth, east_halo(depth_plane))
    dsh[2] = west_of(depth, west_halo(depth_plane))
    dsh[3] = north_of(depth, north_halo(depth_plane))
    dsh[4] = south_of(depth, south_halo(depth_plane))

    for k in range(layer_total):
        for src, dst, base in ((t_ref, tsh, 0), (s_ref, ssh, layer_total)):
            x = src[k]
            dst[0, k] = east_of(x, east_halo(base + k))
            dst[1, k] = west_of(x, west_halo(base + k))
            dst[2, k] = north_of(x, north_halo(base + k))
            dst[3, k] = south_of(x, south_halo(base + k))
        x = u_ref[k]
        ush[0, k] = east_of(x, east_halo(depth_plane + 1 + k))
        ush[1, k] = west_of(x, west_halo(depth_plane + 1 + k))
        x = v_ref[k]
        vsh[0, k] = north_of(x, north_halo(depth_plane + 1 + k))
        vsh[1, k] = south_of(x, south_halo(depth_plane + 1 + k))

    def planes(k):
        at = jnp.clip(k, 0, layer_total - 1)
        temp = [t_ref[at]] + [tsh[i, at] for i in range(4)]
        salt = [s_ref[at]] + [ssh[i, at] for i in range(4)]
        rho = [HALINE * sv - THERMAL * tv for tv, sv in zip(temp, salt)]
        return temp, salt, rho

    def wet_at(k):
        inside = jnp.logical_and(k >= 0, k < layer_total)
        level = k.astype(jnp.float32)
        return [
            jnp.where(jnp.logical_and(inside, level < dsh[i]), 1.0, 0.0) for i in range(5)
        ]

    def horizontal(fields, kcs, wet, a, b, speed_a, speed_b, slope_of):
        face = wet[a] * wet[b]
        temp, salt, rho = fields
        k_temp, k_salt, k_rho = kcs
        slope = jnp.clip(
            -((rho[b] - rho[a]) * face)
            / jnp.maximum(0.5 * (k_rho[a] + k_rho[b]), DENSITY_FLOOR),
            -SLOPE_LIMIT,
            SLOPE_LIMIT,
        )
        flow = 0.5 * (speed_a + speed_b) * face
        up, down = jnp.maximum(flow, 0.0), jnp.minimum(flow, 0.0)
        out = []
        for x, kx in ((temp, k_temp), (salt, k_salt)):
            grad = (x[b] - x[a]) * face
            out.append(
                up * x[a] + down * x[b]
                - DIFFUSIVITY * face * (grad + slope * (0.5 * (kx[a] + kx[b])))
            )
        return out

    def cell_means(x, wet):
        east_grad = (x[1] - x[0]) * (wet[0] * wet[1])
        west_grad = (x[0] - x[2]) * (wet[2] * wet[0])
        north_grad = (x[3] - x[0]) * (wet[0] * wet[3])
        south_grad = (x[0] - x[4]) * (wet[4] * wet[0])
        return 0.5 * (west_grad + east_grad), 0.5 * (south_grad + north_grad)

    def level_step(k, carry):
        down_temp, down_salt = carry
        lower = planes(k - 1)
        here = planes(k)
        upper = planes(k + 1)
        wet_lower = wet_at(k - 1)
        wet_here = wet_at(k)
        wet_upper = wet_at(k + 1)
        face_top = [wet_here[i] * wet_lower[i] for i in range(5)]
        face_bottom = [wet_upper[i] * wet_here[i] for i in range(5)]
        kcs = [
            [
                0.5 * ((h[i] - lo[i]) * face_top[i] + (up[i] - h[i]) * face_bottom[i])
                for i in range(5)
            ]
            for lo, h, up in zip(lower, here, upper)
        ]
        zonal = u_ref[k]
        meridional = v_ref[k]
        east = horizontal(here, kcs, wet_here, 0, 1, zonal, ush[0, k], None)
        west = horizontal(here, kcs, wet_here, 2, 0, ush[1, k], zonal, None)
        north = horizontal(here, kcs, wet_here, 0, 3, meridional, vsh[0, k], None)
        south = horizontal(here, kcs, wet_here, 4, 0, vsh[1, k], meridional, None)
        means_here = [cell_means(f, wet_here) for f in here]
        means_upper = [cell_means(f, wet_upper) for f in upper]
        face = face_bottom[0]
        xu = [0.5 * (mh[0] + mu[0]) for mh, mu in zip(means_here, means_upper)]
        yu = [0.5 * (mh[1] + mu[1]) for mh, mu in zip(means_here, means_upper)]
        dk = [(up[0] - h[0]) * face for h, up in zip(here, upper)]
        floor = jnp.maximum(dk[2], DENSITY_FLOOR)
        slope_x = jnp.clip(-xu[2] / floor, -SLOPE_LIMIT, SLOPE_LIMIT)
        slope_y = jnp.clip(-yu[2] / floor, -SLOPE_LIMIT, SLOPE_LIMIT)
        above = jnp.clip(k + 1, 0, layer_total - 1)
        flow = 0.5 * (w_ref[k] + w_ref[above]) * face
        up, down = jnp.maximum(flow, 0.0), jnp.minimum(flow, 0.0)
        squares = slope_x * slope_x + slope_y * slope_y
        below = []
        for n in range(2):
            below.append(
                up * here[n][0] + down * upper[n][0]
                - DIFFUSIVITY * face * (slope_x * xu[n] + slope_y * yu[n] + squares * dk[n])
            )
        for n, (dst, top) in enumerate(((ot_ref, down_temp), (os_ref, down_salt))):
            divergence = (east[n] - west[n]) + (north[n] - south[n])
            divergence = divergence + (below[n] - top)
            dst[k] = here[n][0] - divergence
        return tuple(below)

    zero = jnp.zeros((rows, cols), jnp.float32)
    lax.fori_loop(0, layer_total, level_step, (zero, zero))


def edge_kernel(
    flag_ref, t_ref, s_ref, u_ref, v_ref, d_ref, west_ref, east_ref, first_ref, second_ref
):
    layer_total, rows, cols = t_ref.shape
    lane_tile = west_ref.shape[1]
    odd = flag_ref[0] == 1
    depth = (d_ref[0] * d_ref[1]).astype(jnp.float32)
    lane = lax.broadcasted_iota(jnp.int32, (rows, lane_tile), 1)
    column_planes = (
        [t_ref[k] for k in range(layer_total)]
        + [s_ref[k] for k in range(layer_total)]
        + [depth]
        + [u_ref[k] for k in range(layer_total)]
    )
    west = jnp.zeros((rows, lane_tile), jnp.float32)
    east = jnp.zeros((rows, lane_tile), jnp.float32)
    for p, x in enumerate(column_planes):
        west = jnp.where(lane == p, x[:, cols - 1 :], west)
        east = jnp.where(lane == p, x[:, :1], east)
    west_ref[...] = west
    east_ref[...] = east
    row_planes = column_planes[: 2 * layer_total + 1] + [v_ref[k] for k in range(layer_total)]
    for p, x in enumerate(row_planes):
        top = x[rows - 1 :, :]
        bottom = x[:1, :]
        first_ref[p : p + 1, :] = jnp.where(odd, top, bottom)
        second_ref[p : p + 1, :] = jnp.where(odd, bottom, top)


def on_device(
    potential_warmth,
    saltiness_anomaly,
    zonal_speed,
    meridional_speed,
    sinking_speed,
    water_indicator,
    seabed_layer_index,
):
    layer_total, rows, cols = potential_warmth.shape
    base_planes = 2 * layer_total + 1
    halo_planes = 3 * layer_total + 1
    lane_tile = 128
    lon_count = lax.axis_size("lon")
    lat_count = lax.axis_size("lat")
    lat_index = lax.axis_index("lat")
    odd = lat_index % 2
    flag = jnp.full((1,), odd, jnp.int32)
    columns = jnp.stack([water_indicator, seabed_layer_index])
    vmem = pltpu.MemorySpace.VMEM
    smem = pltpu.MemorySpace.SMEM
    packed = jax.ShapeDtypeStruct((rows, lane_tile), jnp.float32)
    lines = jax.ShapeDtypeStruct((halo_planes, cols), jnp.float32)
    west_pack, east_pack, first_lines, second_lines = pl.pallas_call(
        edge_kernel,
        out_shape=(packed, packed, lines, lines),
        in_specs=[pl.BlockSpec(memory_space=smem)] + [pl.BlockSpec(memory_space=vmem)] * 5,
        out_specs=tuple(pl.BlockSpec(memory_space=vmem) for _ in range(4)),
    )(flag, potential_warmth, saltiness_anomaly, zonal_speed, meridional_speed, columns)

    west_cols = lax.ppermute(
        west_pack, "lon", [(i, (i + 1) % lon_count) for i in range(lon_count)]
    )
    east_cols = lax.ppermute(
        east_pack, "lon", [((i + 1) % lon_count, i) for i in range(lon_count)]
    )

    def device(lat, lon):
        return lon * lat_count + lat

    first_pairs = []
    second_pairs = []
    for lon in range(lon_count):
        for lat in range(lat_count - 1):
            pairs = first_pairs if lat % 2 else second_pairs
            pairs.append((device(lat, lon), device(lat + 1, lon)))
            pairs.append((device(lat + 1, lon), device(lat, lon)))
        first_pairs.append(
            (device(lat_count - 1, lon), device(lat_count - 1, lon_count - 1 - lon))
        )
    first_got = lax.ppermute(first_lines, ("lon", "lat"), first_pairs)
    second_got = lax.ppermute(second_lines, ("lon", "lat"), second_pairs)
    mirrored = first_got[:, ::-1]
    folded = jnp.concatenate([mirrored[:base_planes], -mirrored[base_planes:]], 0)
    top_row = lat_index == lat_count - 1
    north_rows = jnp.where(odd == 0, second_got, jnp.where(top_row, folded, first_got))
    south_rows = jnp.where(odd == 1, second_got, first_got)

    field = jax.ShapeDtypeStruct(potential_warmth.shape, jnp.float32)
    return pl.pallas_call(
        stencil_kernel,
        out_shape=(field, field),
        in_specs=[pl.BlockSpec(memory_space=vmem)] * 10,
        out_specs=(pl.BlockSpec(memory_space=vmem), pl.BlockSpec(memory_space=vmem)),
        scratch_shapes=[
            pltpu.VMEM((4, layer_total, rows, cols), jnp.float32),
            pltpu.VMEM((4, layer_total, rows, cols), jnp.float32),
            pltpu.VMEM((2, layer_total, rows, cols), jnp.float32),
            pltpu.VMEM((2, layer_total, rows, cols), jnp.float32),
            pltpu.VMEM((5, rows, cols), jnp.float32),
        ],
    )(
        potential_warmth,
        saltiness_anomaly,
        zonal_speed,
        meridional_speed,
        sinking_speed,
        columns,
        west_cols,
        east_cols,
        south_rows,
        north_rows,
    )


def solution(mesh):
    placed = (
        P(None, "lat", "lon"),
        P(None, "lat", "lon"),
        P(None, "lat", "lon"),
        P(None, "lat", "lon"),
        P(None, "lat", "lon"),
        P("lat", "lon"),
        P("lat", "lon"),
    )
    return jax.shard_map(
        on_device,
        mesh=mesh,
        in_specs=placed,
        out_specs=(P(None, "lat", "lon"), P(None, "lat", "lon")),
        check_vma=False,
    )
```

```python
import jax
import jax.numpy as jnp
from jax import lax
from jax.experimental import pallas as pl
from jax.experimental.pallas import tpu as pltpu
from jax.sharding import PartitionSpec as P

DIFFUSIVITY = 0.15
DENSITY_FLOOR = 0.5
SLOPE_LIMIT = 1.0
THERMAL = 0.25
HALINE = 0.75


def stencil_kernel(
    flag_ref, t_ref, s_ref, u_ref, v_ref, w_ref, wi_ref, sb_ref, hw_ref, he_ref,
    first_ref, second_ref, ot_ref, os_ref, tsh, ssh, ush, vsh, dsh,
):
    layer_total, rows, cols = t_ref.shape
    lane = lax.broadcasted_iota(jnp.int32, (rows, cols), 1)
    row = lax.broadcasted_iota(jnp.int32, (rows, cols), 0)
    east_edge = lane == cols - 1
    west_edge = lane == 0
    north_edge = row == rows - 1
    south_edge = row == 0

    def east_of(x, h):
        return jnp.where(east_edge, h, pltpu.roll(x, cols - 1, 1))

    def west_of(x, h):
        return jnp.where(west_edge, h, pltpu.roll(x, 1, 1))

    def north_of(x, h):
        return jnp.where(north_edge, h, pltpu.roll(x, rows - 1, 0))

    def south_of(x, h):
        return jnp.where(south_edge, h, pltpu.roll(x, 1, 0))

    lane_tile = hw_ref.shape[1]

    def column_of(ref, p, at):
        packed = ref[...]
        shift = (at - p) % lane_tile
        if shift:
            packed = pltpu.roll(packed, shift, 1)
        return jnp.concatenate([packed] * (cols // lane_tile), 1)

    def east_halo(p):
        return column_of(he_ref, p, lane_tile - 1)

    def west_halo(p):
        return column_of(hw_ref, p, 0)

    odd = flag_ref[0] == 1

    def north_halo(p):
        return jnp.where(odd, first_ref[p : p + 1, :], second_ref[p : p + 1, :])

    def south_halo(p):
        return jnp.where(odd, second_ref[p : p + 1, :], first_ref[p : p + 1, :])

    depth_plane = 2 * layer_total
    depth = (wi_ref[...] * sb_ref[...]).astype(jnp.float32)
    dsh[0] = depth
    dsh[1] = east_of(depth, east_halo(depth_plane))
    dsh[2] = west_of(depth, west_halo(depth_plane))
    dsh[3] = north_of(depth, north_halo(depth_plane))
    dsh[4] = south_of(depth, south_halo(depth_plane))

    for k in range(layer_total):
        for src, dst, base in ((t_ref, tsh, 0), (s_ref, ssh, layer_total)):
            x = src[k]
            dst[0, k] = east_of(x, east_halo(base + k))
            dst[1, k] = west_of(x, west_halo(base + k))
            dst[2, k] = north_of(x, north_halo(base + k))
            dst[3, k] = south_of(x, south_halo(base + k))
        x = u_ref[k]
        ush[0, k] = east_of(x, east_halo(depth_plane + 1 + k))
        ush[1, k] = west_of(x, west_halo(depth_plane + 1 + k))
        x = v_ref[k]
        vsh[0, k] = north_of(x, north_halo(depth_plane + 1 + k))
        vsh[1, k] = south_of(x, south_halo(depth_plane + 1 + k))

    def planes(k):
        at = jnp.clip(k, 0, layer_total - 1)
        temp = [t_ref[at]] + [tsh[i, at] for i in range(4)]
        salt = [s_ref[at]] + [ssh[i, at] for i in range(4)]
        rho = [HALINE * sv - THERMAL * tv for tv, sv in zip(temp, salt)]
        return temp, salt, rho

    def wet_at(k):
        inside = jnp.logical_and(k >= 0, k < layer_total)
        level = k.astype(jnp.float32)
        return [
            jnp.where(jnp.logical_and(inside, level < dsh[i]), 1.0, 0.0) for i in range(5)
        ]

    def horizontal(fields, kcs, wet, a, b, speed_a, speed_b, slope_of):
        face = wet[a] * wet[b]
        temp, salt, rho = fields
        k_temp, k_salt, k_rho = kcs
        slope = jnp.clip(
            -((rho[b] - rho[a]) * face)
            / jnp.maximum(0.5 * (k_rho[a] + k_rho[b]), DENSITY_FLOOR),
            -SLOPE_LIMIT,
            SLOPE_LIMIT,
        )
        flow = 0.5 * (speed_a + speed_b) * face
        up, down = jnp.maximum(flow, 0.0), jnp.minimum(flow, 0.0)
        out = []
        for x, kx in ((temp, k_temp), (salt, k_salt)):
            grad = (x[b] - x[a]) * face
            out.append(
                up * x[a] + down * x[b]
                - DIFFUSIVITY * face * (grad + slope * (0.5 * (kx[a] + kx[b])))
            )
        return out

    def cell_means(x, wet):
        east_grad = (x[1] - x[0]) * (wet[0] * wet[1])
        west_grad = (x[0] - x[2]) * (wet[2] * wet[0])
        north_grad = (x[3] - x[0]) * (wet[0] * wet[3])
        south_grad = (x[0] - x[4]) * (wet[4] * wet[0])
        return 0.5 * (west_grad + east_grad), 0.5 * (south_grad + north_grad)

    def level_step(k, carry):
        down_temp, down_salt = carry
        lower = planes(k - 1)
        here = planes(k)
        upper = planes(k + 1)
        wet_lower = wet_at(k - 1)
        wet_here = wet_at(k)
        wet_upper = wet_at(k + 1)
        face_top = [wet_here[i] * wet_lower[i] for i in range(5)]
        face_bottom = [wet_upper[i] * wet_here[i] for i in range(5)]
        kcs = [
            [
                0.5 * ((h[i] - lo[i]) * face_top[i] + (up[i] - h[i]) * face_bottom[i])
                for i in range(5)
            ]
            for lo, h, up in zip(lower, here, upper)
        ]
        zonal = u_ref[k]
        meridional = v_ref[k]
        east = horizontal(here, kcs, wet_here, 0, 1, zonal, ush[0, k], None)
        west = horizontal(here, kcs, wet_here, 2, 0, ush[1, k], zonal, None)
        north = horizontal(here, kcs, wet_here, 0, 3, meridional, vsh[0, k], None)
        south = horizontal(here, kcs, wet_here, 4, 0, vsh[1, k], meridional, None)
        means_here = [cell_means(f, wet_here) for f in here]
        means_upper = [cell_means(f, wet_upper) for f in upper]
        face = face_bottom[0]
        xu = [0.5 * (mh[0] + mu[0]) for mh, mu in zip(means_here, means_upper)]
        yu = [0.5 * (mh[1] + mu[1]) for mh, mu in zip(means_here, means_upper)]
        dk = [(up[0] - h[0]) * face for h, up in zip(here, upper)]
        floor = jnp.maximum(dk[2], DENSITY_FLOOR)
        slope_x = jnp.clip(-xu[2] / floor, -SLOPE_LIMIT, SLOPE_LIMIT)
        slope_y = jnp.clip(-yu[2] / floor, -SLOPE_LIMIT, SLOPE_LIMIT)
        above = jnp.clip(k + 1, 0, layer_total - 1)
        flow = 0.5 * (w_ref[k] + w_ref[above]) * face
        up, down = jnp.maximum(flow, 0.0), jnp.minimum(flow, 0.0)
        squares = slope_x * slope_x + slope_y * slope_y
        below = []
        for n in range(2):
            below.append(
                up * here[n][0] + down * upper[n][0]
                - DIFFUSIVITY * face * (slope_x * xu[n] + slope_y * yu[n] + squares * dk[n])
            )
        for n, (dst, top) in enumerate(((ot_ref, down_temp), (os_ref, down_salt))):
            divergence = (east[n] - west[n]) + (north[n] - south[n])
            divergence = divergence + (below[n] - top)
            dst[k] = here[n][0] - divergence
        return tuple(below)

    zero = jnp.zeros((rows, cols), jnp.float32)
    lax.fori_loop(0, layer_total, level_step, (zero, zero))


def edge_kernel(
    flag_ref, t_ref, s_ref, u_ref, v_ref, wi_ref, sb_ref,
    west_ref, east_ref, first_ref, second_ref, tops_ref, bottoms_ref,
):
    layer_total, rows, cols = t_ref.shape
    lane_tile = west_ref.shape[1]
    odd = flag_ref[0] == 1
    top = flag_ref[1] == 1
    depth = (wi_ref[...] * sb_ref[...]).astype(jnp.float32)
    lane = lax.broadcasted_iota(jnp.int32, (rows, lane_tile), 1)
    column_planes = (
        [t_ref[k] for k in range(layer_total)]
        + [s_ref[k] for k in range(layer_total)]
        + [depth]
        + [u_ref[k] for k in range(layer_total)]
    )
    west = jnp.zeros((rows, lane_tile), jnp.float32)
    east = jnp.zeros((rows, lane_tile), jnp.float32)
    for p, x in enumerate(column_planes):
        west = jnp.where(lane == p, x[:, cols - 1 :], west)
        east = jnp.where(lane == p, x[:, :1], east)
    west_ref[...] = west
    east_ref[...] = east
    base_planes = 2 * layer_total + 1
    row_planes = column_planes[:base_planes] + [v_ref[k] for k in range(layer_total)]
    for p, x in enumerate(row_planes):
        tops_ref[p : p + 1, :] = x[rows - 1 :, :]
        bottoms_ref[p : p + 1, :] = x[:1, :]
    tops = tops_ref[...]
    bottoms = bottoms_ref[...]
    line_lane = lax.broadcasted_iota(jnp.int32, tops.shape, 1)
    mirrored = tops
    step = 1
    while step < cols:
        mirrored = jnp.where(
            (line_lane & step) != 0,
            pltpu.roll(mirrored, step, 1),
            pltpu.roll(mirrored, cols - step, 1),
        )
        step *= 2
    plane = lax.broadcasted_iota(jnp.int32, tops.shape, 0)
    folded = jnp.where(plane >= base_planes, -mirrored, mirrored)
    first_ref[...] = jnp.where(top, folded, jnp.where(odd, tops, bottoms))
    second_ref[...] = jnp.where(odd, bottoms, tops)


def on_device(
    potential_warmth,
    saltiness_anomaly,
    zonal_speed,
    meridional_speed,
    sinking_speed,
    water_indicator,
    seabed_layer_index,
):
    layer_total, rows, cols = potential_warmth.shape
    base_planes = 2 * layer_total + 1
    halo_planes = 3 * layer_total + 1
    lane_tile = 128
    lon_count = lax.axis_size("lon")
    lat_count = lax.axis_size("lat")
    lat_index = lax.axis_index("lat")
    odd = lat_index % 2
    top_row = lat_index == lat_count - 1
    flag = jnp.stack([odd, top_row.astype(jnp.int32)]).astype(jnp.int32)
    vmem = pltpu.MemorySpace.VMEM
    smem = pltpu.MemorySpace.SMEM
    packed = jax.ShapeDtypeStruct((rows, lane_tile), jnp.float32)
    lines = jax.ShapeDtypeStruct((halo_planes, cols), jnp.float32)
    west_pack, east_pack, first_lines, second_lines = pl.pallas_call(
        edge_kernel,
        out_shape=(packed, packed, lines, lines),
        in_specs=[pl.BlockSpec(memory_space=smem)] + [pl.BlockSpec(memory_space=vmem)] * 6,
        out_specs=tuple(pl.BlockSpec(memory_space=vmem) for _ in range(4)),
        scratch_shapes=[
            pltpu.VMEM((halo_planes, cols), jnp.float32),
            pltpu.VMEM((halo_planes, cols), jnp.float32),
        ],
    )(
        flag,
        potential_warmth,
        saltiness_anomaly,
        zonal_speed,
        meridional_speed,
        water_indicator,
        seabed_layer_index,
    )

    west_cols = lax.ppermute(
        west_pack, "lon", [(i, (i + 1) % lon_count) for i in range(lon_count)]
    )
    east_cols = lax.ppermute(
        east_pack, "lon", [((i + 1) % lon_count, i) for i in range(lon_count)]
    )

    def device(lat, lon):
        return lon * lat_count + lat

    first_pairs = []
    second_pairs = []
    for lon in range(lon_count):
        for lat in range(lat_count - 1):
            pairs = first_pairs if lat % 2 else second_pairs
            pairs.append((device(lat, lon), device(lat + 1, lon)))
            pairs.append((device(lat + 1, lon), device(lat, lon)))
        first_pairs.append(
            (device(lat_count - 1, lon), device(lat_count - 1, lon_count - 1 - lon))
        )
    first_got = lax.ppermute(first_lines, ("lon", "lat"), first_pairs)
    second_got = lax.ppermute(second_lines, ("lon", "lat"), second_pairs)
    field = jax.ShapeDtypeStruct(potential_warmth.shape, jnp.float32)
    return pl.pallas_call(
        stencil_kernel,
        out_shape=(field, field),
        in_specs=[pl.BlockSpec(memory_space=smem)] + [pl.BlockSpec(memory_space=vmem)] * 11,
        out_specs=(pl.BlockSpec(memory_space=vmem), pl.BlockSpec(memory_space=vmem)),
        scratch_shapes=[
            pltpu.VMEM((4, layer_total, rows, cols), jnp.float32),
            pltpu.VMEM((4, layer_total, rows, cols), jnp.float32),
            pltpu.VMEM((2, layer_total, rows, cols), jnp.float32),
            pltpu.VMEM((2, layer_total, rows, cols), jnp.float32),
            pltpu.VMEM((5, rows, cols), jnp.float32),
        ],
    )(
        flag,
        potential_warmth,
        saltiness_anomaly,
        zonal_speed,
        meridional_speed,
        sinking_speed,
        water_indicator,
        seabed_layer_index,
        west_cols,
        east_cols,
        first_got,
        second_got,
    )


def solution(mesh):
    placed = (
        P(None, "lat", "lon"),
        P(None, "lat", "lon"),
        P(None, "lat", "lon"),
        P(None, "lat", "lon"),
        P(None, "lat", "lon"),
        P("lat", "lon"),
        P("lat", "lon"),
    )
    return jax.shard_map(
        on_device,
        mesh=mesh,
        in_specs=placed,
        out_specs=(P(None, "lat", "lon"), P(None, "lat", "lon")),
        check_vma=False,
    )
```

```python
import jax
import jax.numpy as jnp
from jax import lax
from jax.experimental import pallas as pl
from jax.experimental.pallas import tpu as pltpu
from jax.sharding import PartitionSpec as P

DIFFUSIVITY = 0.15
DENSITY_FLOOR = 0.5
SLOPE_LIMIT = 1.0
THERMAL = 0.25
HALINE = 0.75


def stencil_kernel(
    flag_ref, t_ref, s_ref, u_ref, v_ref, w_ref, wi_ref, sb_ref, hw_ref, he_ref,
    first_ref, second_ref, ot_ref, os_ref, tsh, ssh, ush, vsh, dsh,
):
    layer_total, rows, cols = t_ref.shape
    lane = lax.broadcasted_iota(jnp.int32, (rows, cols), 1)
    row = lax.broadcasted_iota(jnp.int32, (rows, cols), 0)
    east_edge = lane == cols - 1
    west_edge = lane == 0
    north_edge = row == rows - 1
    south_edge = row == 0

    def east_of(x, h):
        return jnp.where(east_edge, h, pltpu.roll(x, cols - 1, 1))

    def west_of(x, h):
        return jnp.where(west_edge, h, pltpu.roll(x, 1, 1))

    def north_of(x, h):
        return jnp.where(north_edge, h, pltpu.roll(x, rows - 1, 0))

    def south_of(x, h):
        return jnp.where(south_edge, h, pltpu.roll(x, 1, 0))

    lane_tile = hw_ref.shape[1]

    def column_of(ref, p, at):
        packed = ref[...]
        shift = (at - p) % lane_tile
        if shift:
            packed = pltpu.roll(packed, shift, 1)
        return jnp.concatenate([packed] * (cols // lane_tile), 1)

    def east_halo(p):
        return column_of(he_ref, p, lane_tile - 1)

    def west_halo(p):
        return column_of(hw_ref, p, 0)

    odd = flag_ref[0] == 1

    def north_halo(p):
        return jnp.where(odd, first_ref[p : p + 1, :], second_ref[p : p + 1, :])

    def south_halo(p):
        return jnp.where(odd, second_ref[p : p + 1, :], first_ref[p : p + 1, :])

    depth_plane = 2 * layer_total
    depth = (wi_ref[...] * sb_ref[...]).astype(jnp.float32)
    dsh[0] = depth
    dsh[1] = east_of(depth, east_halo(depth_plane))
    dsh[2] = west_of(depth, west_halo(depth_plane))
    dsh[3] = north_of(depth, north_halo(depth_plane))
    dsh[4] = south_of(depth, south_halo(depth_plane))

    for k in range(layer_total):
        for src, dst, base in ((t_ref, tsh, 0), (s_ref, ssh, layer_total)):
            x = src[k]
            dst[0, k] = east_of(x, east_halo(base + k))
            dst[1, k] = west_of(x, west_halo(base + k))
            dst[2, k] = north_of(x, north_halo(base + k))
            dst[3, k] = south_of(x, south_halo(base + k))
        x = u_ref[k]
        ush[0, k] = east_of(x, east_halo(depth_plane + 1 + k))
        ush[1, k] = west_of(x, west_halo(depth_plane + 1 + k))
        x = v_ref[k]
        vsh[0, k] = north_of(x, north_halo(depth_plane + 1 + k))
        vsh[1, k] = south_of(x, south_halo(depth_plane + 1 + k))

    def planes(k):
        at = jnp.clip(k, 0, layer_total - 1)
        temp = [t_ref[at]] + [tsh[i, at] for i in range(4)]
        salt = [s_ref[at]] + [ssh[i, at] for i in range(4)]
        rho = [HALINE * sv - THERMAL * tv for tv, sv in zip(temp, salt)]
        return temp, salt, rho

    def wet_at(k):
        inside = jnp.logical_and(k >= 0, k < layer_total)
        level = k.astype(jnp.float32)
        return [
            jnp.where(jnp.logical_and(inside, level < dsh[i]), 1.0, 0.0) for i in range(5)
        ]

    sub_tile = 8

    def whole(x):
        return x

    def west_part(x):
        return x[:, :lane_tile]

    def south_part(x):
        return x[:sub_tile, :]

    def horizontal(fields, kcs, wet, a, b, speed_a, speed_b, part):
        face = part(wet[a]) * part(wet[b])
        temp, salt, rho = fields
        k_temp, k_salt, k_rho = kcs
        slope = jnp.clip(
            -((part(rho[b]) - part(rho[a])) * face)
            / jnp.maximum(0.5 * (k_rho[a] + k_rho[b]), DENSITY_FLOOR),
            -SLOPE_LIMIT,
            SLOPE_LIMIT,
        )
        flow = 0.5 * (part(speed_a) + part(speed_b)) * face
        up, down = jnp.maximum(flow, 0.0), jnp.minimum(flow, 0.0)
        out = []
        for x, kx in ((temp, k_temp), (salt, k_salt)):
            xa, xb = part(x[a]), part(x[b])
            grad = (xb - xa) * face
            out.append(
                up * xa + down * xb
                - DIFFUSIVITY * face * (grad + slope * (0.5 * (kx[a] + kx[b])))
            )
        return out

    def cell_means(x, wet):
        east_grad = (x[1] - x[0]) * (wet[0] * wet[1])
        west_grad = (x[0] - x[2]) * (wet[2] * wet[0])
        north_grad = (x[3] - x[0]) * (wet[0] * wet[3])
        south_grad = (x[0] - x[4]) * (wet[4] * wet[0])
        return 0.5 * (west_grad + east_grad), 0.5 * (south_grad + north_grad)

    def vertical_mean(lo, h, up, face_top, face_bottom, i, part):
        return 0.5 * (
            (part(h[i]) - part(lo[i])) * part(face_top[i])
            + (part(up[i]) - part(h[i])) * part(face_bottom[i])
        )

    def level_step(k, carry):
        down_temp, down_salt = carry
        lower = planes(k - 1)
        here = planes(k)
        upper = planes(k + 1)
        wet_lower = wet_at(k - 1)
        wet_here = wet_at(k)
        wet_upper = wet_at(k + 1)
        face_top = [wet_here[i] * wet_lower[i] for i in range(5)]
        face_bottom = [wet_upper[i] * wet_here[i] for i in range(5)]

        def kc_set(i, part):
            return [
                vertical_mean(lo, h, up, face_top, face_bottom, i, part)
                for lo, h, up in zip(lower, here, upper)
            ]

        kc_full = [kc_set(i, whole) for i in (0, 1, 3)]
        kcs = [[kc_full[0][n], kc_full[1][n], None, kc_full[2][n], None] for n in range(3)]
        west_kcs = [[kc_set(0, west_part)[n], None, kc_set(2, west_part)[n], None, None] for n in range(3)]
        south_kcs = [[kc_set(0, south_part)[n], None, None, None, kc_set(4, south_part)[n]] for n in range(3)]
        zonal = u_ref[k]
        meridional = v_ref[k]
        east = horizontal(here, kcs, wet_here, 0, 1, zonal, ush[0, k], whole)
        west_edge_flux = horizontal(here, west_kcs, wet_here, 2, 0, ush[1, k], zonal, west_part)
        north = horizontal(here, kcs, wet_here, 0, 3, meridional, vsh[0, k], whole)
        south_edge_flux = horizontal(
            here, south_kcs, wet_here, 4, 0, vsh[1, k], meridional, south_part
        )
        west = [
            jnp.where(
                west_edge,
                jnp.concatenate([w] * (cols // lane_tile), 1),
                pltpu.roll(f, 1, 1),
            )
            for w, f in zip(west_edge_flux, east)
        ]
        south = [
            jnp.where(
                south_edge,
                jnp.concatenate([s] * (rows // sub_tile), 0),
                pltpu.roll(f, 1, 0),
            )
            for s, f in zip(south_edge_flux, north)
        ]
        means_here = [cell_means(f, wet_here) for f in here]
        means_upper = [cell_means(f, wet_upper) for f in upper]
        face = face_bottom[0]
        xu = [0.5 * (mh[0] + mu[0]) for mh, mu in zip(means_here, means_upper)]
        yu = [0.5 * (mh[1] + mu[1]) for mh, mu in zip(means_here, means_upper)]
        dk = [(up[0] - h[0]) * face for h, up in zip(here, upper)]
        floor = jnp.maximum(dk[2], DENSITY_FLOOR)
        slope_x = jnp.clip(-xu[2] / floor, -SLOPE_LIMIT, SLOPE_LIMIT)
        slope_y = jnp.clip(-yu[2] / floor, -SLOPE_LIMIT, SLOPE_LIMIT)
        above = jnp.clip(k + 1, 0, layer_total - 1)
        flow = 0.5 * (w_ref[k] + w_ref[above]) * face
        up, down = jnp.maximum(flow, 0.0), jnp.minimum(flow, 0.0)
        squares = slope_x * slope_x + slope_y * slope_y
        below = []
        for n in range(2):
            below.append(
                up * here[n][0] + down * upper[n][0]
                - DIFFUSIVITY * face * (slope_x * xu[n] + slope_y * yu[n] + squares * dk[n])
            )
        for n, (dst, top) in enumerate(((ot_ref, down_temp), (os_ref, down_salt))):
            divergence = (east[n] - west[n]) + (north[n] - south[n])
            divergence = divergence + (below[n] - top)
            dst[k] = here[n][0] - divergence
        return tuple(below)

    zero = jnp.zeros((rows, cols), jnp.float32)
    lax.fori_loop(0, layer_total, level_step, (zero, zero))


def edge_kernel(
    flag_ref, t_ref, s_ref, u_ref, v_ref, wi_ref, sb_ref,
    west_ref, east_ref, first_ref, second_ref, tops_ref, bottoms_ref,
):
    layer_total, rows, cols = t_ref.shape
    lane_tile = west_ref.shape[1]
    odd = flag_ref[0] == 1
    top = flag_ref[1] == 1
    depth = (wi_ref[...] * sb_ref[...]).astype(jnp.float32)
    lane = lax.broadcasted_iota(jnp.int32, (rows, lane_tile), 1)
    column_planes = (
        [t_ref[k] for k in range(layer_total)]
        + [s_ref[k] for k in range(layer_total)]
        + [depth]
        + [u_ref[k] for k in range(layer_total)]
    )
    west = jnp.zeros((rows, lane_tile), jnp.float32)
    east = jnp.zeros((rows, lane_tile), jnp.float32)
    for p, x in enumerate(column_planes):
        west = jnp.where(lane == p, x[:, cols - 1 :], west)
        east = jnp.where(lane == p, x[:, :1], east)
    west_ref[...] = west
    east_ref[...] = east
    base_planes = 2 * layer_total + 1
    row_planes = column_planes[:base_planes] + [v_ref[k] for k in range(layer_total)]
    for p, x in enumerate(row_planes):
        tops_ref[p : p + 1, :] = x[rows - 1 :, :]
        bottoms_ref[p : p + 1, :] = x[:1, :]
    tops = tops_ref[...]
    bottoms = bottoms_ref[...]
    line_lane = lax.broadcasted_iota(jnp.int32, tops.shape, 1)
    mirrored = tops
    step = 1
    while step < cols:
        mirrored = jnp.where(
            (line_lane & step) != 0,
            pltpu.roll(mirrored, step, 1),
            pltpu.roll(mirrored, cols - step, 1),
        )
        step *= 2
    plane = lax.broadcasted_iota(jnp.int32, tops.shape, 0)
    folded = jnp.where(plane >= base_planes, -mirrored, mirrored)
    first_ref[...] = jnp.where(top, folded, jnp.where(odd, tops, bottoms))
    second_ref[...] = jnp.where(odd, bottoms, tops)


def on_device(
    potential_warmth,
    saltiness_anomaly,
    zonal_speed,
    meridional_speed,
    sinking_speed,
    water_indicator,
    seabed_layer_index,
):
    layer_total, rows, cols = potential_warmth.shape
    base_planes = 2 * layer_total + 1
    halo_planes = 3 * layer_total + 1
    lane_tile = 128
    lon_count = lax.axis_size("lon")
    lat_count = lax.axis_size("lat")
    lat_index = lax.axis_index("lat")
    odd = lat_index % 2
    top_row = lat_index == lat_count - 1
    flag = jnp.stack([odd, top_row.astype(jnp.int32)]).astype(jnp.int32)
    vmem = pltpu.MemorySpace.VMEM
    smem = pltpu.MemorySpace.SMEM
    packed = jax.ShapeDtypeStruct((rows, lane_tile), jnp.float32)
    lines = jax.ShapeDtypeStruct((halo_planes, cols), jnp.float32)
    west_pack, east_pack, first_lines, second_lines = pl.pallas_call(
        edge_kernel,
        out_shape=(packed, packed, lines, lines),
        in_specs=[pl.BlockSpec(memory_space=smem)] + [pl.BlockSpec(memory_space=vmem)] * 6,
        out_specs=tuple(pl.BlockSpec(memory_space=vmem) for _ in range(4)),
        scratch_shapes=[
            pltpu.VMEM((halo_planes, cols), jnp.float32),
            pltpu.VMEM((halo_planes, cols), jnp.float32),
        ],
    )(
        flag,
        potential_warmth,
        saltiness_anomaly,
        zonal_speed,
        meridional_speed,
        water_indicator,
        seabed_layer_index,
    )

    west_cols = lax.ppermute(
        west_pack, "lon", [(i, (i + 1) % lon_count) for i in range(lon_count)]
    )
    east_cols = lax.ppermute(
        east_pack, "lon", [((i + 1) % lon_count, i) for i in range(lon_count)]
    )

    def device(lat, lon):
        return lon * lat_count + lat

    first_pairs = []
    second_pairs = []
    for lon in range(lon_count):
        for lat in range(lat_count - 1):
            pairs = first_pairs if lat % 2 else second_pairs
            pairs.append((device(lat, lon), device(lat + 1, lon)))
            pairs.append((device(lat + 1, lon), device(lat, lon)))
        first_pairs.append(
            (device(lat_count - 1, lon), device(lat_count - 1, lon_count - 1 - lon))
        )
    first_got = lax.ppermute(first_lines, ("lon", "lat"), first_pairs)
    second_got = lax.ppermute(second_lines, ("lon", "lat"), second_pairs)
    field = jax.ShapeDtypeStruct(potential_warmth.shape, jnp.float32)
    return pl.pallas_call(
        stencil_kernel,
        out_shape=(field, field),
        in_specs=[pl.BlockSpec(memory_space=smem)] + [pl.BlockSpec(memory_space=vmem)] * 11,
        out_specs=(pl.BlockSpec(memory_space=vmem), pl.BlockSpec(memory_space=vmem)),
        scratch_shapes=[
            pltpu.VMEM((4, layer_total, rows, cols), jnp.float32),
            pltpu.VMEM((4, layer_total, rows, cols), jnp.float32),
            pltpu.VMEM((2, layer_total, rows, cols), jnp.float32),
            pltpu.VMEM((2, layer_total, rows, cols), jnp.float32),
            pltpu.VMEM((5, rows, cols), jnp.float32),
        ],
    )(
        flag,
        potential_warmth,
        saltiness_anomaly,
        zonal_speed,
        meridional_speed,
        sinking_speed,
        water_indicator,
        seabed_layer_index,
        west_cols,
        east_cols,
        first_got,
        second_got,
    )


def solution(mesh):
    placed = (
        P(None, "lat", "lon"),
        P(None, "lat", "lon"),
        P(None, "lat", "lon"),
        P(None, "lat", "lon"),
        P(None, "lat", "lon"),
        P("lat", "lon"),
        P("lat", "lon"),
    )
    return jax.shard_map(
        on_device,
        mesh=mesh,
        in_specs=placed,
        out_specs=(P(None, "lat", "lon"), P(None, "lat", "lon")),
        check_vma=False,
    )
```

```python
import jax
import jax.numpy as jnp
from jax import lax
from jax.experimental import pallas as pl
from jax.experimental.pallas import tpu as pltpu
from jax.sharding import PartitionSpec as P

DIFFUSIVITY = 0.15
DENSITY_FLOOR = 0.5
SLOPE_LIMIT = 1.0
THERMAL = 0.25
HALINE = 0.75


def stencil_kernel(
    flag_ref, t_hbm, s_hbm, u_hbm, v_hbm, w_hbm, wi_ref, sb_ref, hw_hbm, he_hbm,
    first_hbm, second_hbm, ot_ref, os_ref, tsh, ssh, ush, vsh, dsh,
    t_ref, s_ref, u_ref, v_ref, w_ref, hw_ref, he_ref, first_ref, second_ref, sems,
):
    layer_total, rows, cols = t_ref.shape
    copies = [
        pltpu.make_async_copy(source, target, sems.at[n])
        for n, (source, target) in enumerate(
            (
                (hw_hbm, hw_ref),
                (he_hbm, he_ref),
                (first_hbm, first_ref),
                (second_hbm, second_ref),
                (t_hbm, t_ref),
                (s_hbm, s_ref),
                (u_hbm, u_ref),
                (v_hbm, v_ref),
                (w_hbm, w_ref),
            )
        )
    ]
    for copy in copies:
        copy.start()
    for copy in copies[:6]:
        copy.wait()
    lane = lax.broadcasted_iota(jnp.int32, (rows, cols), 1)
    row = lax.broadcasted_iota(jnp.int32, (rows, cols), 0)
    east_edge = lane == cols - 1
    west_edge = lane == 0
    north_edge = row == rows - 1
    south_edge = row == 0

    def east_of(x, h):
        return jnp.where(east_edge, h, pltpu.roll(x, cols - 1, 1))

    def west_of(x, h):
        return jnp.where(west_edge, h, pltpu.roll(x, 1, 1))

    def north_of(x, h):
        return jnp.where(north_edge, h, pltpu.roll(x, rows - 1, 0))

    def south_of(x, h):
        return jnp.where(south_edge, h, pltpu.roll(x, 1, 0))

    lane_tile = hw_ref.shape[1]

    def column_of(ref, p, at):
        packed = ref[...]
        shift = (at - p) % lane_tile
        if shift:
            packed = pltpu.roll(packed, shift, 1)
        return jnp.concatenate([packed] * (cols // lane_tile), 1)

    def east_halo(p):
        return column_of(he_ref, p, lane_tile - 1)

    def west_halo(p):
        return column_of(hw_ref, p, 0)

    odd = flag_ref[0] == 1

    def north_halo(p):
        return jnp.where(odd, first_ref[p : p + 1, :], second_ref[p : p + 1, :])

    def south_halo(p):
        return jnp.where(odd, second_ref[p : p + 1, :], first_ref[p : p + 1, :])

    depth_plane = 2 * layer_total
    depth = (wi_ref[...] * sb_ref[...]).astype(jnp.float32)
    dsh[0] = depth
    dsh[1] = east_of(depth, east_halo(depth_plane))
    dsh[2] = west_of(depth, west_halo(depth_plane))
    dsh[3] = north_of(depth, north_halo(depth_plane))
    dsh[4] = south_of(depth, south_halo(depth_plane))

    for k in range(layer_total):
        for src, dst, base in ((t_ref, tsh, 0), (s_ref, ssh, layer_total)):
            x = src[k]
            dst[0, k] = east_of(x, east_halo(base + k))
            dst[1, k] = west_of(x, west_halo(base + k))
            dst[2, k] = north_of(x, north_halo(base + k))
            dst[3, k] = south_of(x, south_halo(base + k))
    copies[6].wait()
    copies[7].wait()
    for k in range(layer_total):
        x = u_ref[k]
        ush[0, k] = east_of(x, east_halo(depth_plane + 1 + k))
        ush[1, k] = west_of(x, west_halo(depth_plane + 1 + k))
        x = v_ref[k]
        vsh[0, k] = north_of(x, north_halo(depth_plane + 1 + k))
        vsh[1, k] = south_of(x, south_halo(depth_plane + 1 + k))

    def planes(k):
        at = jnp.clip(k, 0, layer_total - 1)
        temp = [t_ref[at]] + [tsh[i, at] for i in range(4)]
        salt = [s_ref[at]] + [ssh[i, at] for i in range(4)]
        rho = [HALINE * sv - THERMAL * tv for tv, sv in zip(temp, salt)]
        return temp, salt, rho

    def wet_at(k):
        inside = jnp.logical_and(k >= 0, k < layer_total)
        level = k.astype(jnp.float32)
        return [
            jnp.where(jnp.logical_and(inside, level < dsh[i]), 1.0, 0.0) for i in range(5)
        ]

    sub_tile = 8

    def whole(x):
        return x

    def west_part(x):
        return x[:, :lane_tile]

    def south_part(x):
        return x[:sub_tile, :]

    def horizontal(fields, kcs, wet, a, b, speed_a, speed_b, part):
        face = part(wet[a]) * part(wet[b])
        temp, salt, rho = fields
        k_temp, k_salt, k_rho = kcs
        slope = jnp.clip(
            -((part(rho[b]) - part(rho[a])) * face)
            / jnp.maximum(0.5 * (k_rho[a] + k_rho[b]), DENSITY_FLOOR),
            -SLOPE_LIMIT,
            SLOPE_LIMIT,
        )
        flow = 0.5 * (part(speed_a) + part(speed_b)) * face
        up, down = jnp.maximum(flow, 0.0), jnp.minimum(flow, 0.0)
        out = []
        for x, kx in ((temp, k_temp), (salt, k_salt)):
            xa, xb = part(x[a]), part(x[b])
            grad = (xb - xa) * face
            out.append(
                up * xa + down * xb
                - DIFFUSIVITY * face * (grad + slope * (0.5 * (kx[a] + kx[b])))
            )
        return out

    def cell_means(x, wet):
        east_grad = (x[1] - x[0]) * (wet[0] * wet[1])
        west_grad = (x[0] - x[2]) * (wet[2] * wet[0])
        north_grad = (x[3] - x[0]) * (wet[0] * wet[3])
        south_grad = (x[0] - x[4]) * (wet[4] * wet[0])
        return 0.5 * (west_grad + east_grad), 0.5 * (south_grad + north_grad)

    def vertical_mean(lo, h, up, face_top, face_bottom, i, part):
        return 0.5 * (
            (part(h[i]) - part(lo[i])) * part(face_top[i])
            + (part(up[i]) - part(h[i])) * part(face_bottom[i])
        )

    def level_step(k, carry):
        down_temp, down_salt = carry
        lower = planes(k - 1)
        here = planes(k)
        upper = planes(k + 1)
        wet_lower = wet_at(k - 1)
        wet_here = wet_at(k)
        wet_upper = wet_at(k + 1)
        face_top = [wet_here[i] * wet_lower[i] for i in range(5)]
        face_bottom = [wet_upper[i] * wet_here[i] for i in range(5)]

        def kc_set(i, part):
            return [
                vertical_mean(lo, h, up, face_top, face_bottom, i, part)
                for lo, h, up in zip(lower, here, upper)
            ]

        kc_full = [kc_set(i, whole) for i in (0, 1, 3)]
        kcs = [[kc_full[0][n], kc_full[1][n], None, kc_full[2][n], None] for n in range(3)]
        west_kcs = [[kc_set(0, west_part)[n], None, kc_set(2, west_part)[n], None, None] for n in range(3)]
        south_kcs = [[kc_set(0, south_part)[n], None, None, None, kc_set(4, south_part)[n]] for n in range(3)]
        zonal = u_ref[k]
        meridional = v_ref[k]
        east = horizontal(here, kcs, wet_here, 0, 1, zonal, ush[0, k], whole)
        west_edge_flux = horizontal(here, west_kcs, wet_here, 2, 0, ush[1, k], zonal, west_part)
        north = horizontal(here, kcs, wet_here, 0, 3, meridional, vsh[0, k], whole)
        south_edge_flux = horizontal(
            here, south_kcs, wet_here, 4, 0, vsh[1, k], meridional, south_part
        )
        west = [
            jnp.where(
                west_edge,
                jnp.concatenate([w] * (cols // lane_tile), 1),
                pltpu.roll(f, 1, 1),
            )
            for w, f in zip(west_edge_flux, east)
        ]
        south = [
            jnp.where(
                south_edge,
                jnp.concatenate([s] * (rows // sub_tile), 0),
                pltpu.roll(f, 1, 0),
            )
            for s, f in zip(south_edge_flux, north)
        ]
        means_here = [cell_means(f, wet_here) for f in here]
        means_upper = [cell_means(f, wet_upper) for f in upper]
        face = face_bottom[0]
        xu = [0.5 * (mh[0] + mu[0]) for mh, mu in zip(means_here, means_upper)]
        yu = [0.5 * (mh[1] + mu[1]) for mh, mu in zip(means_here, means_upper)]
        dk = [(up[0] - h[0]) * face for h, up in zip(here, upper)]
        floor = jnp.maximum(dk[2], DENSITY_FLOOR)
        slope_x = jnp.clip(-xu[2] / floor, -SLOPE_LIMIT, SLOPE_LIMIT)
        slope_y = jnp.clip(-yu[2] / floor, -SLOPE_LIMIT, SLOPE_LIMIT)
        above = jnp.clip(k + 1, 0, layer_total - 1)
        flow = 0.5 * (w_ref[k] + w_ref[above]) * face
        up, down = jnp.maximum(flow, 0.0), jnp.minimum(flow, 0.0)
        squares = slope_x * slope_x + slope_y * slope_y
        below = []
        for n in range(2):
            below.append(
                up * here[n][0] + down * upper[n][0]
                - DIFFUSIVITY * face * (slope_x * xu[n] + slope_y * yu[n] + squares * dk[n])
            )
        for n, (dst, top) in enumerate(((ot_ref, down_temp), (os_ref, down_salt))):
            divergence = (east[n] - west[n]) + (north[n] - south[n])
            divergence = divergence + (below[n] - top)
            dst[k] = here[n][0] - divergence
        return tuple(below)

    copies[8].wait()
    zero = jnp.zeros((rows, cols), jnp.float32)
    lax.fori_loop(0, layer_total, level_step, (zero, zero))


def edge_kernel(
    flag_ref, t_ref, s_ref, u_ref, v_ref, wi_ref, sb_ref,
    west_ref, east_ref, first_ref, second_ref, tops_ref, bottoms_ref,
):
    layer_total, rows, cols = t_ref.shape
    lane_tile = west_ref.shape[1]
    odd = flag_ref[0] == 1
    top = flag_ref[1] == 1
    depth = (wi_ref[...] * sb_ref[...]).astype(jnp.float32)
    lane = lax.broadcasted_iota(jnp.int32, (rows, lane_tile), 1)
    column_planes = (
        [t_ref[k] for k in range(layer_total)]
        + [s_ref[k] for k in range(layer_total)]
        + [depth]
        + [u_ref[k] for k in range(layer_total)]
    )
    west = jnp.zeros((rows, lane_tile), jnp.float32)
    east = jnp.zeros((rows, lane_tile), jnp.float32)
    for p, x in enumerate(column_planes):
        west = jnp.where(lane == p, x[:, cols - 1 :], west)
        east = jnp.where(lane == p, x[:, :1], east)
    west_ref[...] = west
    east_ref[...] = east
    base_planes = 2 * layer_total + 1
    row_planes = column_planes[:base_planes] + [v_ref[k] for k in range(layer_total)]
    for p, x in enumerate(row_planes):
        tops_ref[p : p + 1, :] = x[rows - 1 :, :]
        bottoms_ref[p : p + 1, :] = x[:1, :]
    tops = tops_ref[...]
    bottoms = bottoms_ref[...]
    line_lane = lax.broadcasted_iota(jnp.int32, tops.shape, 1)
    mirrored = tops
    step = 1
    while step < cols:
        mirrored = jnp.where(
            (line_lane & step) != 0,
            pltpu.roll(mirrored, step, 1),
            pltpu.roll(mirrored, cols - step, 1),
        )
        step *= 2
    plane = lax.broadcasted_iota(jnp.int32, tops.shape, 0)
    folded = jnp.where(plane >= base_planes, -mirrored, mirrored)
    first_ref[...] = jnp.where(top, folded, jnp.where(odd, tops, bottoms))
    second_ref[...] = jnp.where(odd, bottoms, tops)


def on_device(
    potential_warmth,
    saltiness_anomaly,
    zonal_speed,
    meridional_speed,
    sinking_speed,
    water_indicator,
    seabed_layer_index,
):
    layer_total, rows, cols = potential_warmth.shape
    base_planes = 2 * layer_total + 1
    halo_planes = 3 * layer_total + 1
    lane_tile = 128
    lon_count = lax.axis_size("lon")
    lat_count = lax.axis_size("lat")
    lat_index = lax.axis_index("lat")
    odd = lat_index % 2
    top_row = lat_index == lat_count - 1
    flag = jnp.stack([odd, top_row.astype(jnp.int32)]).astype(jnp.int32)
    vmem = pltpu.MemorySpace.VMEM
    smem = pltpu.MemorySpace.SMEM
    packed = jax.ShapeDtypeStruct((rows, lane_tile), jnp.float32)
    lines = jax.ShapeDtypeStruct((halo_planes, cols), jnp.float32)
    west_pack, east_pack, first_lines, second_lines = pl.pallas_call(
        edge_kernel,
        out_shape=(packed, packed, lines, lines),
        in_specs=[pl.BlockSpec(memory_space=smem)] + [pl.BlockSpec(memory_space=vmem)] * 6,
        out_specs=tuple(pl.BlockSpec(memory_space=vmem) for _ in range(4)),
        scratch_shapes=[
            pltpu.VMEM((halo_planes, cols), jnp.float32),
            pltpu.VMEM((halo_planes, cols), jnp.float32),
        ],
    )(
        flag,
        potential_warmth,
        saltiness_anomaly,
        zonal_speed,
        meridional_speed,
        water_indicator,
        seabed_layer_index,
    )

    west_cols = lax.ppermute(
        west_pack, "lon", [(i, (i + 1) % lon_count) for i in range(lon_count)]
    )
    east_cols = lax.ppermute(
        east_pack, "lon", [((i + 1) % lon_count, i) for i in range(lon_count)]
    )

    def device(lat, lon):
        return lon * lat_count + lat

    first_pairs = []
    second_pairs = []
    for lon in range(lon_count):
        for lat in range(lat_count - 1):
            pairs = first_pairs if lat % 2 else second_pairs
            pairs.append((device(lat, lon), device(lat + 1, lon)))
            pairs.append((device(lat + 1, lon), device(lat, lon)))
        first_pairs.append(
            (device(lat_count - 1, lon), device(lat_count - 1, lon_count - 1 - lon))
        )
    first_got = lax.ppermute(first_lines, ("lon", "lat"), first_pairs)
    second_got = lax.ppermute(second_lines, ("lon", "lat"), second_pairs)
    field = jax.ShapeDtypeStruct(potential_warmth.shape, jnp.float32)
    return pl.pallas_call(
        stencil_kernel,
        out_shape=(field, field),
        in_specs=[pl.BlockSpec(memory_space=smem)]
        + [pl.BlockSpec(memory_space=pl.ANY)] * 5
        + [pl.BlockSpec(memory_space=vmem)] * 2
        + [pl.BlockSpec(memory_space=pl.ANY)] * 4,
        out_specs=(pl.BlockSpec(memory_space=vmem), pl.BlockSpec(memory_space=vmem)),
        scratch_shapes=[
            pltpu.VMEM((4, layer_total, rows, cols), jnp.float32),
            pltpu.VMEM((4, layer_total, rows, cols), jnp.float32),
            pltpu.VMEM((2, layer_total, rows, cols), jnp.float32),
            pltpu.VMEM((2, layer_total, rows, cols), jnp.float32),
            pltpu.VMEM((5, rows, cols), jnp.float32),
        ]
        + [pltpu.VMEM(potential_warmth.shape, jnp.float32)] * 5
        + [pltpu.VMEM(west_cols.shape, jnp.float32)] * 2
        + [pltpu.VMEM(first_got.shape, jnp.float32)] * 2
        + [pltpu.SemaphoreType.DMA((9,))],
    )(
        flag,
        potential_warmth,
        saltiness_anomaly,
        zonal_speed,
        meridional_speed,
        sinking_speed,
        water_indicator,
        seabed_layer_index,
        west_cols,
        east_cols,
        first_got,
        second_got,
    )


def solution(mesh):
    placed = (
        P(None, "lat", "lon"),
        P(None, "lat", "lon"),
        P(None, "lat", "lon"),
        P(None, "lat", "lon"),
        P(None, "lat", "lon"),
        P("lat", "lon"),
        P("lat", "lon"),
    )
    return jax.shard_map(
        on_device,
        mesh=mesh,
        in_specs=placed,
        out_specs=(P(None, "lat", "lon"), P(None, "lat", "lon")),
        check_vma=False,
    )
```

```python
import jax
import jax.numpy as jnp
from jax import lax
from jax.experimental import pallas as pl
from jax.experimental.pallas import tpu as pltpu
from jax.sharding import PartitionSpec as P

DIFFUSIVITY = 0.15
DENSITY_FLOOR = 0.5
SLOPE_LIMIT = 1.0
THERMAL = 0.25
HALINE = 0.75


def stencil_kernel(
    t_ref, s_ref, u_ref, v_ref, w_ref, wi_ref, sb_ref, hw_ref, he_ref,
    first_ref, second_ref, ot_ref, os_ref, tsh, ssh, ush, vsh, dsh,
):
    layer_total, rows, cols = t_ref.shape
    lane = lax.broadcasted_iota(jnp.int32, (rows, cols), 1)
    row = lax.broadcasted_iota(jnp.int32, (rows, cols), 0)
    east_edge = lane == cols - 1
    west_edge = lane == 0
    north_edge = row == rows - 1
    south_edge = row == 0

    def east_of(x, h):
        return jnp.where(east_edge, h, pltpu.roll(x, cols - 1, 1))

    def west_of(x, h):
        return jnp.where(west_edge, h, pltpu.roll(x, 1, 1))

    def north_of(x, h):
        return jnp.where(north_edge, h, pltpu.roll(x, rows - 1, 0))

    def south_of(x, h):
        return jnp.where(south_edge, h, pltpu.roll(x, 1, 0))

    lane_tile = hw_ref.shape[1]

    def column_of(ref, p, at):
        packed = ref[...]
        shift = (at - p) % lane_tile
        if shift:
            packed = pltpu.roll(packed, shift, 1)
        return jnp.concatenate([packed] * (cols // lane_tile), 1)

    def east_halo(p):
        return column_of(he_ref, p, lane_tile - 1)

    def west_halo(p):
        return column_of(hw_ref, p, 0)

    odd = lax.axis_index("lat") % 2 == 1

    def north_halo(p):
        return jnp.where(odd, first_ref[p : p + 1, :], second_ref[p : p + 1, :])

    def south_halo(p):
        return jnp.where(odd, second_ref[p : p + 1, :], first_ref[p : p + 1, :])

    depth_plane = 2 * layer_total
    depth = (wi_ref[...] * sb_ref[...]).astype(jnp.float32)
    dsh[0] = depth
    dsh[1] = east_of(depth, east_halo(depth_plane))
    dsh[2] = west_of(depth, west_halo(depth_plane))
    dsh[3] = north_of(depth, north_halo(depth_plane))
    dsh[4] = south_of(depth, south_halo(depth_plane))

    for k in range(layer_total):
        for src, dst, base in ((t_ref, tsh, 0), (s_ref, ssh, layer_total)):
            x = src[k]
            dst[0, k] = east_of(x, east_halo(base + k))
            dst[1, k] = west_of(x, west_halo(base + k))
            dst[2, k] = north_of(x, north_halo(base + k))
            dst[3, k] = south_of(x, south_halo(base + k))
        x = u_ref[k]
        ush[0, k] = east_of(x, east_halo(depth_plane + 1 + k))
        ush[1, k] = west_of(x, west_halo(depth_plane + 1 + k))
        x = v_ref[k]
        vsh[0, k] = north_of(x, north_halo(depth_plane + 1 + k))
        vsh[1, k] = south_of(x, south_halo(depth_plane + 1 + k))

    def planes(k):
        at = jnp.clip(k, 0, layer_total - 1)
        temp = [t_ref[at]] + [tsh[i, at] for i in range(4)]
        salt = [s_ref[at]] + [ssh[i, at] for i in range(4)]
        rho = [HALINE * sv - THERMAL * tv for tv, sv in zip(temp, salt)]
        return temp, salt, rho

    def wet_at(k):
        inside = jnp.logical_and(k >= 0, k < layer_total)
        level = k.astype(jnp.float32)
        return [
            jnp.where(jnp.logical_and(inside, level < dsh[i]), 1.0, 0.0) for i in range(5)
        ]

    sub_tile = 8

    def whole(x):
        return x

    def west_part(x):
        return x[:, :lane_tile]

    def south_part(x):
        return x[:sub_tile, :]

    def horizontal(fields, kcs, wet, a, b, speed_a, speed_b, part):
        face = part(wet[a]) * part(wet[b])
        temp, salt, rho = fields
        k_temp, k_salt, k_rho = kcs
        slope = jnp.clip(
            -((part(rho[b]) - part(rho[a])) * face)
            / jnp.maximum(0.5 * (k_rho[a] + k_rho[b]), DENSITY_FLOOR),
            -SLOPE_LIMIT,
            SLOPE_LIMIT,
        )
        flow = 0.5 * (part(speed_a) + part(speed_b)) * face
        up, down = jnp.maximum(flow, 0.0), jnp.minimum(flow, 0.0)
        out = []
        for x, kx in ((temp, k_temp), (salt, k_salt)):
            xa, xb = part(x[a]), part(x[b])
            grad = (xb - xa) * face
            out.append(
                up * xa + down * xb
                - DIFFUSIVITY * face * (grad + slope * (0.5 * (kx[a] + kx[b])))
            )
        return out

    def cell_means(x, wet):
        east_grad = (x[1] - x[0]) * (wet[0] * wet[1])
        west_grad = (x[0] - x[2]) * (wet[2] * wet[0])
        north_grad = (x[3] - x[0]) * (wet[0] * wet[3])
        south_grad = (x[0] - x[4]) * (wet[4] * wet[0])
        return 0.5 * (west_grad + east_grad), 0.5 * (south_grad + north_grad)

    def vertical_mean(lo, h, up, face_top, face_bottom, i, part):
        return 0.5 * (
            (part(h[i]) - part(lo[i])) * part(face_top[i])
            + (part(up[i]) - part(h[i])) * part(face_bottom[i])
        )

    def level_step(k, carry):
        down_temp, down_salt = carry
        lower = planes(k - 1)
        here = planes(k)
        upper = planes(k + 1)
        wet_lower = wet_at(k - 1)
        wet_here = wet_at(k)
        wet_upper = wet_at(k + 1)
        face_top = [wet_here[i] * wet_lower[i] for i in range(5)]
        face_bottom = [wet_upper[i] * wet_here[i] for i in range(5)]

        def kc_set(i, part):
            return [
                vertical_mean(lo, h, up, face_top, face_bottom, i, part)
                for lo, h, up in zip(lower, here, upper)
            ]

        kc_full = [kc_set(i, whole) for i in (0, 1, 3)]
        kcs = [[kc_full[0][n], kc_full[1][n], None, kc_full[2][n], None] for n in range(3)]
        west_kcs = [[kc_set(0, west_part)[n], None, kc_set(2, west_part)[n], None, None] for n in range(3)]
        south_kcs = [[kc_set(0, south_part)[n], None, None, None, kc_set(4, south_part)[n]] for n in range(3)]
        zonal = u_ref[k]
        meridional = v_ref[k]
        east = horizontal(here, kcs, wet_here, 0, 1, zonal, ush[0, k], whole)
        west_edge_flux = horizontal(here, west_kcs, wet_here, 2, 0, ush[1, k], zonal, west_part)
        north = horizontal(here, kcs, wet_here, 0, 3, meridional, vsh[0, k], whole)
        south_edge_flux = horizontal(
            here, south_kcs, wet_here, 4, 0, vsh[1, k], meridional, south_part
        )
        west = [
            jnp.where(
                west_edge,
                jnp.concatenate([w] * (cols // lane_tile), 1),
                pltpu.roll(f, 1, 1),
            )
            for w, f in zip(west_edge_flux, east)
        ]
        south = [
            jnp.where(
                south_edge,
                jnp.concatenate([s] * (rows // sub_tile), 0),
                pltpu.roll(f, 1, 0),
            )
            for s, f in zip(south_edge_flux, north)
        ]
        means_here = [cell_means(f, wet_here) for f in here]
        means_upper = [cell_means(f, wet_upper) for f in upper]
        face = face_bottom[0]
        xu = [0.5 * (mh[0] + mu[0]) for mh, mu in zip(means_here, means_upper)]
        yu = [0.5 * (mh[1] + mu[1]) for mh, mu in zip(means_here, means_upper)]
        dk = [(up[0] - h[0]) * face for h, up in zip(here, upper)]
        floor = jnp.maximum(dk[2], DENSITY_FLOOR)
        slope_x = jnp.clip(-xu[2] / floor, -SLOPE_LIMIT, SLOPE_LIMIT)
        slope_y = jnp.clip(-yu[2] / floor, -SLOPE_LIMIT, SLOPE_LIMIT)
        above = jnp.clip(k + 1, 0, layer_total - 1)
        flow = 0.5 * (w_ref[k] + w_ref[above]) * face
        up, down = jnp.maximum(flow, 0.0), jnp.minimum(flow, 0.0)
        squares = slope_x * slope_x + slope_y * slope_y
        below = []
        for n in range(2):
            below.append(
                up * here[n][0] + down * upper[n][0]
                - DIFFUSIVITY * face * (slope_x * xu[n] + slope_y * yu[n] + squares * dk[n])
            )
        for n, (dst, top) in enumerate(((ot_ref, down_temp), (os_ref, down_salt))):
            divergence = (east[n] - west[n]) + (north[n] - south[n])
            divergence = divergence + (below[n] - top)
            dst[k] = here[n][0] - divergence
        return tuple(below)

    zero = jnp.zeros((rows, cols), jnp.float32)
    lax.fori_loop(0, layer_total, level_step, (zero, zero))


def edge_kernel(
    t_ref, s_ref, u_ref, v_ref, wi_ref, sb_ref,
    west_ref, east_ref, first_ref, second_ref, tops_ref, bottoms_ref,
):
    layer_total, rows, cols = t_ref.shape
    lane_tile = west_ref.shape[1]
    lat_index = lax.axis_index("lat")
    odd = lat_index % 2 == 1
    top = lat_index == lax.axis_size("lat") - 1
    depth = (wi_ref[...] * sb_ref[...]).astype(jnp.float32)
    lane = lax.broadcasted_iota(jnp.int32, (rows, lane_tile), 1)
    column_planes = (
        [t_ref[k] for k in range(layer_total)]
        + [s_ref[k] for k in range(layer_total)]
        + [depth]
        + [u_ref[k] for k in range(layer_total)]
    )
    west = jnp.zeros((rows, lane_tile), jnp.float32)
    east = jnp.zeros((rows, lane_tile), jnp.float32)
    for p, x in enumerate(column_planes):
        west = jnp.where(lane == p, x[:, cols - 1 :], west)
        east = jnp.where(lane == p, x[:, :1], east)
    west_ref[...] = west
    east_ref[...] = east
    base_planes = 2 * layer_total + 1
    row_planes = column_planes[:base_planes] + [v_ref[k] for k in range(layer_total)]
    for p, x in enumerate(row_planes):
        tops_ref[p : p + 1, :] = x[rows - 1 :, :]
        bottoms_ref[p : p + 1, :] = x[:1, :]
    tops = tops_ref[...]
    bottoms = bottoms_ref[...]
    line_lane = lax.broadcasted_iota(jnp.int32, tops.shape, 1)
    mirrored = tops
    step = 1
    while step < cols:
        mirrored = jnp.where(
            (line_lane & step) != 0,
            pltpu.roll(mirrored, step, 1),
            pltpu.roll(mirrored, cols - step, 1),
        )
        step *= 2
    plane = lax.broadcasted_iota(jnp.int32, tops.shape, 0)
    folded = jnp.where(plane >= base_planes, -mirrored, mirrored)
    first_ref[...] = jnp.where(top, folded, jnp.where(odd, tops, bottoms))
    second_ref[...] = jnp.where(odd, bottoms, tops)


def on_device(
    potential_warmth,
    saltiness_anomaly,
    zonal_speed,
    meridional_speed,
    sinking_speed,
    water_indicator,
    seabed_layer_index,
):
    layer_total, rows, cols = potential_warmth.shape
    base_planes = 2 * layer_total + 1
    halo_planes = 3 * layer_total + 1
    lane_tile = 128
    lon_count = lax.axis_size("lon")
    lat_count = lax.axis_size("lat")
    lat_index = lax.axis_index("lat")
    odd = lat_index % 2
    vmem = pltpu.MemorySpace.VMEM
    smem = pltpu.MemorySpace.SMEM
    packed = jax.ShapeDtypeStruct((rows, lane_tile), jnp.float32)
    lines = jax.ShapeDtypeStruct((halo_planes, cols), jnp.float32)
    west_pack, east_pack, first_lines, second_lines = pl.pallas_call(
        edge_kernel,
        out_shape=(packed, packed, lines, lines),
        in_specs=[pl.BlockSpec(memory_space=vmem)] * 6,
        out_specs=tuple(pl.BlockSpec(memory_space=vmem) for _ in range(4)),
        scratch_shapes=[
            pltpu.VMEM((halo_planes, cols), jnp.float32),
            pltpu.VMEM((halo_planes, cols), jnp.float32),
        ],
    )(
        potential_warmth,
        saltiness_anomaly,
        zonal_speed,
        meridional_speed,
        water_indicator,
        seabed_layer_index,
    )

    west_cols = lax.ppermute(
        west_pack, "lon", [(i, (i + 1) % lon_count) for i in range(lon_count)]
    )
    east_cols = lax.ppermute(
        east_pack, "lon", [((i + 1) % lon_count, i) for i in range(lon_count)]
    )

    def device(lat, lon):
        return lon * lat_count + lat

    first_pairs = []
    second_pairs = []
    for lon in range(lon_count):
        for lat in range(lat_count - 1):
            pairs = first_pairs if lat % 2 else second_pairs
            pairs.append((device(lat, lon), device(lat + 1, lon)))
            pairs.append((device(lat + 1, lon), device(lat, lon)))
        first_pairs.append(
            (device(lat_count - 1, lon), device(lat_count - 1, lon_count - 1 - lon))
        )
    first_got = lax.ppermute(first_lines, ("lon", "lat"), first_pairs)
    second_got = lax.ppermute(second_lines, ("lon", "lat"), second_pairs)
    field = jax.ShapeDtypeStruct(potential_warmth.shape, jnp.float32)
    return pl.pallas_call(
        stencil_kernel,
        out_shape=(field, field),
        in_specs=[pl.BlockSpec(memory_space=vmem)] * 11,
        out_specs=(pl.BlockSpec(memory_space=vmem), pl.BlockSpec(memory_space=vmem)),
        scratch_shapes=[
            pltpu.VMEM((4, layer_total, rows, cols), jnp.float32),
            pltpu.VMEM((4, layer_total, rows, cols), jnp.float32),
            pltpu.VMEM((2, layer_total, rows, cols), jnp.float32),
            pltpu.VMEM((2, layer_total, rows, cols), jnp.float32),
            pltpu.VMEM((5, rows, cols), jnp.float32),
        ],
    )(
        potential_warmth,
        saltiness_anomaly,
        zonal_speed,
        meridional_speed,
        sinking_speed,
        water_indicator,
        seabed_layer_index,
        west_cols,
        east_cols,
        first_got,
        second_got,
    )


def solution(mesh):
    placed = (
        P(None, "lat", "lon"),
        P(None, "lat", "lon"),
        P(None, "lat", "lon"),
        P(None, "lat", "lon"),
        P(None, "lat", "lon"),
        P("lat", "lon"),
        P("lat", "lon"),
    )
    return jax.shard_map(
        on_device,
        mesh=mesh,
        in_specs=placed,
        out_specs=(P(None, "lat", "lon"), P(None, "lat", "lon")),
        check_vma=False,
    )
```

```python
import jax
import jax.numpy as jnp
from jax import lax
from jax.experimental import pallas as pl
from jax.experimental.pallas import tpu as pltpu
from jax.sharding import PartitionSpec as P

DIFFUSIVITY = 0.15
DENSITY_FLOOR = 0.5
SLOPE_LIMIT = 1.0
THERMAL = 0.25
HALINE = 0.75


def stencil_kernel(
    t_ref, s_ref, u_ref, v_ref, w_ref, wi_ref, sb_ref, hw_ref, he_ref,
    first_ref, second_ref, ot_ref, os_ref, tsh, ssh, ush, vsh, dsh,
):
    layer_total, rows, cols = t_ref.shape
    lane = lax.broadcasted_iota(jnp.int32, (rows, cols), 1)
    row = lax.broadcasted_iota(jnp.int32, (rows, cols), 0)
    east_edge = lane == cols - 1
    west_edge = lane == 0
    north_edge = row == rows - 1
    south_edge = row == 0

    def east_of(x, h):
        return jnp.where(east_edge, h, pltpu.roll(x, cols - 1, 1))

    def west_of(x, h):
        return jnp.where(west_edge, h, pltpu.roll(x, 1, 1))

    def north_of(x, h):
        return jnp.where(north_edge, h, pltpu.roll(x, rows - 1, 0))

    def south_of(x, h):
        return jnp.where(south_edge, h, pltpu.roll(x, 1, 0))

    lane_tile = hw_ref.shape[1]

    def column_of(ref, p, at):
        packed = ref[...]
        shift = (at - p) % lane_tile
        if shift:
            packed = pltpu.roll(packed, shift, 1)
        return jnp.concatenate([packed] * (cols // lane_tile), 1)

    def east_halo(p):
        return column_of(he_ref, p, lane_tile - 1)

    def west_halo(p):
        return column_of(hw_ref, p, 0)

    odd = lax.axis_index("lat") % 2 == 1

    def north_halo(p):
        return jnp.where(odd, first_ref[p : p + 1, :], second_ref[p : p + 1, :])

    def south_halo(p):
        return jnp.where(odd, second_ref[p : p + 1, :], first_ref[p : p + 1, :])

    depth_plane = 2 * layer_total
    depth = (wi_ref[...] * sb_ref[...]).astype(jnp.float32)
    dsh[0] = depth
    dsh[1] = east_of(depth, east_halo(depth_plane))
    dsh[2] = west_of(depth, west_halo(depth_plane))
    dsh[3] = north_of(depth, north_halo(depth_plane))
    dsh[4] = south_of(depth, south_halo(depth_plane))

    for k in range(layer_total):
        for src, dst, base in ((t_ref, tsh, 0), (s_ref, ssh, layer_total)):
            x = src[k]
            dst[0, k] = east_of(x, east_halo(base + k))
            dst[1, k] = west_of(x, west_halo(base + k))
            dst[2, k] = north_of(x, north_halo(base + k))
            dst[3, k] = south_of(x, south_halo(base + k))
        x = u_ref[k]
        ush[0, k] = east_of(x, east_halo(depth_plane + 1 + k))
        ush[1, k] = west_of(x, west_halo(depth_plane + 1 + k))
        x = v_ref[k]
        vsh[0, k] = north_of(x, north_halo(depth_plane + 1 + k))
        vsh[1, k] = south_of(x, south_halo(depth_plane + 1 + k))

    def planes(k):
        at = jnp.clip(k, 0, layer_total - 1)
        temp = [t_ref[at]] + [tsh[i, at] for i in range(4)]
        salt = [s_ref[at]] + [ssh[i, at] for i in range(4)]
        rho = [HALINE * sv - THERMAL * tv for tv, sv in zip(temp, salt)]
        return temp, salt, rho

    def wet_at(k):
        inside = jnp.logical_and(k >= 0, k < layer_total)
        level = k.astype(jnp.float32)
        return [
            jnp.where(jnp.logical_and(inside, level < dsh[i]), 1.0, 0.0) for i in range(5)
        ]

    sub_tile = 8

    def whole(x):
        return x

    def west_part(x):
        return x[:, :lane_tile]

    def south_part(x):
        return x[:sub_tile, :]

    def horizontal(fields, kcs, wet, a, b, speed_a, speed_b, part):
        face = part(wet[a]) * part(wet[b])
        temp, salt, rho = fields
        k_temp, k_salt, k_rho = kcs
        slope = jnp.clip(
            -((part(rho[b]) - part(rho[a])) * face)
            / jnp.maximum(0.5 * (k_rho[a] + k_rho[b]), DENSITY_FLOOR),
            -SLOPE_LIMIT,
            SLOPE_LIMIT,
        )
        flow = 0.5 * (part(speed_a) + part(speed_b)) * face
        up, down = jnp.maximum(flow, 0.0), jnp.minimum(flow, 0.0)
        out = []
        for x, kx in ((temp, k_temp), (salt, k_salt)):
            xa, xb = part(x[a]), part(x[b])
            grad = (xb - xa) * face
            out.append(
                up * xa + down * xb
                - DIFFUSIVITY * face * (grad + slope * (0.5 * (kx[a] + kx[b])))
            )
        return out

    def cell_means(x, wet):
        east_grad = (x[1] - x[0]) * (wet[0] * wet[1])
        west_grad = (x[0] - x[2]) * (wet[2] * wet[0])
        north_grad = (x[3] - x[0]) * (wet[0] * wet[3])
        south_grad = (x[0] - x[4]) * (wet[4] * wet[0])
        return 0.5 * (west_grad + east_grad), 0.5 * (south_grad + north_grad)

    def vertical_mean(lo, h, up, face_top, face_bottom, i, part):
        return 0.5 * (
            (part(h[i]) - part(lo[i])) * part(face_top[i])
            + (part(up[i]) - part(h[i])) * part(face_bottom[i])
        )

    def level_step(k, carry):
        down_temp, down_salt = carry
        lower = planes(k - 1)
        here = planes(k)
        upper = planes(k + 1)
        wet_lower = wet_at(k - 1)
        wet_here = wet_at(k)
        wet_upper = wet_at(k + 1)
        face_top = [wet_here[i] * wet_lower[i] for i in range(5)]
        face_bottom = [wet_upper[i] * wet_here[i] for i in range(5)]

        def kc_set(i, part):
            return [
                vertical_mean(lo, h, up, face_top, face_bottom, i, part)
                for lo, h, up in zip(lower, here, upper)
            ]

        kc_full = [kc_set(i, whole) for i in (0, 1, 3)]
        kcs = [[kc_full[0][n], kc_full[1][n], None, kc_full[2][n], None] for n in range(3)]
        west_kcs = [[kc_set(0, west_part)[n], None, kc_set(2, west_part)[n], None, None] for n in range(3)]
        south_kcs = [[kc_set(0, south_part)[n], None, None, None, kc_set(4, south_part)[n]] for n in range(3)]
        zonal = u_ref[k]
        meridional = v_ref[k]
        east = horizontal(here, kcs, wet_here, 0, 1, zonal, ush[0, k], whole)
        west_edge_flux = horizontal(here, west_kcs, wet_here, 2, 0, ush[1, k], zonal, west_part)
        north = horizontal(here, kcs, wet_here, 0, 3, meridional, vsh[0, k], whole)
        south_edge_flux = horizontal(
            here, south_kcs, wet_here, 4, 0, vsh[1, k], meridional, south_part
        )
        west = [
            jnp.where(
                west_edge,
                jnp.concatenate([w] * (cols // lane_tile), 1),
                pltpu.roll(f, 1, 1),
            )
            for w, f in zip(west_edge_flux, east)
        ]
        south = [
            jnp.where(
                south_edge,
                jnp.concatenate([s] * (rows // sub_tile), 0),
                pltpu.roll(f, 1, 0),
            )
            for s, f in zip(south_edge_flux, north)
        ]
        means_here = [cell_means(f, wet_here) for f in here]
        means_upper = [cell_means(f, wet_upper) for f in upper]
        face = face_bottom[0]
        xu = [0.5 * (mh[0] + mu[0]) for mh, mu in zip(means_here, means_upper)]
        yu = [0.5 * (mh[1] + mu[1]) for mh, mu in zip(means_here, means_upper)]
        dk = [(up[0] - h[0]) * face for h, up in zip(here, upper)]
        floor = jnp.maximum(dk[2], DENSITY_FLOOR)
        slope_x = jnp.clip(-xu[2] / floor, -SLOPE_LIMIT, SLOPE_LIMIT)
        slope_y = jnp.clip(-yu[2] / floor, -SLOPE_LIMIT, SLOPE_LIMIT)
        above = jnp.clip(k + 1, 0, layer_total - 1)
        flow = 0.5 * (w_ref[k] + w_ref[above]) * face
        up, down = jnp.maximum(flow, 0.0), jnp.minimum(flow, 0.0)
        squares = slope_x * slope_x + slope_y * slope_y
        below = []
        for n in range(2):
            below.append(
                up * here[n][0] + down * upper[n][0]
                - DIFFUSIVITY * face * (slope_x * xu[n] + slope_y * yu[n] + squares * dk[n])
            )
        for n, (dst, top) in enumerate(((ot_ref, down_temp), (os_ref, down_salt))):
            divergence = (east[n] - west[n]) + (north[n] - south[n])
            divergence = divergence + (below[n] - top)
            dst[k] = here[n][0] - divergence
        return tuple(below)

    zero = jnp.zeros((rows, cols), jnp.float32)
    lax.fori_loop(0, layer_total, level_step, (zero, zero))


def edge_kernel(
    t_hbm, s_hbm, u_hbm, v_hbm, wi_ref, sb_ref,
    west_ref, east_ref, first_ref, second_ref, tops_ref, bottoms_ref,
    t_ref, s_ref, u_ref, v_ref, sems,
):
    layer_total, rows, cols = t_ref.shape
    copies = [
        pltpu.make_async_copy(source, target, sems.at[n])
        for n, (source, target) in enumerate(
            ((t_hbm, t_ref), (s_hbm, s_ref), (u_hbm, u_ref), (v_hbm, v_ref))
        )
    ]
    for copy in copies:
        copy.start()
    lane_tile = west_ref.shape[1]
    lat_index = lax.axis_index("lat")
    odd = lat_index % 2 == 1
    top = lat_index == lax.axis_size("lat") - 1
    depth = (wi_ref[...] * sb_ref[...]).astype(jnp.float32)
    lane = lax.broadcasted_iota(jnp.int32, (rows, lane_tile), 1)
    west = jnp.zeros((rows, lane_tile), jnp.float32)
    east = jnp.zeros((rows, lane_tile), jnp.float32)

    def edges(x, p, west, east, column, line):
        if column:
            west = jnp.where(lane == p, x[:, cols - 1 :], west)
            east = jnp.where(lane == p, x[:, :1], east)
        if line:
            tops_ref[p : p + 1, :] = x[rows - 1 :, :]
            bottoms_ref[p : p + 1, :] = x[:1, :]
        return west, east

    base_planes = 2 * layer_total + 1
    sources = ((t_ref, 0, True, True), (s_ref, layer_total, True, True))
    for n, (ref, base, column, line) in enumerate(sources):
        copies[n].wait()
        for k in range(layer_total):
            west, east = edges(ref[k], base + k, west, east, column, line)
    west, east = edges(depth, base_planes - 1, west, east, True, True)
    copies[2].wait()
    for k in range(layer_total):
        west, east = edges(u_ref[k], base_planes + k, west, east, True, False)
    west_ref[...] = west
    east_ref[...] = east
    copies[3].wait()
    for k in range(layer_total):
        west, east = edges(v_ref[k], base_planes + k, west, east, False, True)
    tops = tops_ref[...]
    bottoms = bottoms_ref[...]
    line_lane = lax.broadcasted_iota(jnp.int32, tops.shape, 1)
    mirrored = tops
    step = 1
    while step < cols:
        mirrored = jnp.where(
            (line_lane & step) != 0,
            pltpu.roll(mirrored, step, 1),
            pltpu.roll(mirrored, cols - step, 1),
        )
        step *= 2
    plane = lax.broadcasted_iota(jnp.int32, tops.shape, 0)
    folded = jnp.where(plane >= base_planes, -mirrored, mirrored)
    first_ref[...] = jnp.where(top, folded, jnp.where(odd, tops, bottoms))
    second_ref[...] = jnp.where(odd, bottoms, tops)


def on_device(
    potential_warmth,
    saltiness_anomaly,
    zonal_speed,
    meridional_speed,
    sinking_speed,
    water_indicator,
    seabed_layer_index,
):
    layer_total, rows, cols = potential_warmth.shape
    base_planes = 2 * layer_total + 1
    halo_planes = 3 * layer_total + 1
    lane_tile = 128
    lon_count = lax.axis_size("lon")
    lat_count = lax.axis_size("lat")
    lat_index = lax.axis_index("lat")
    odd = lat_index % 2
    vmem = pltpu.MemorySpace.VMEM
    smem = pltpu.MemorySpace.SMEM
    packed = jax.ShapeDtypeStruct((rows, lane_tile), jnp.float32)
    lines = jax.ShapeDtypeStruct((halo_planes, cols), jnp.float32)
    west_pack, east_pack, first_lines, second_lines = pl.pallas_call(
        edge_kernel,
        out_shape=(packed, packed, lines, lines),
        in_specs=[pl.BlockSpec(memory_space=pltpu.MemorySpace.HBM)] * 4
        + [pl.BlockSpec(memory_space=vmem)] * 2,
        out_specs=tuple(pl.BlockSpec(memory_space=vmem) for _ in range(4)),
        scratch_shapes=[
            pltpu.VMEM((halo_planes, cols), jnp.float32),
            pltpu.VMEM((halo_planes, cols), jnp.float32),
        ]
        + [pltpu.VMEM(potential_warmth.shape, jnp.float32)] * 4
        + [pltpu.SemaphoreType.DMA((4,))],
    )(
        potential_warmth,
        saltiness_anomaly,
        zonal_speed,
        meridional_speed,
        water_indicator,
        seabed_layer_index,
    )

    west_cols = lax.ppermute(
        west_pack, "lon", [(i, (i + 1) % lon_count) for i in range(lon_count)]
    )
    east_cols = lax.ppermute(
        east_pack, "lon", [((i + 1) % lon_count, i) for i in range(lon_count)]
    )

    def device(lat, lon):
        return lon * lat_count + lat

    first_pairs = []
    second_pairs = []
    for lon in range(lon_count):
        for lat in range(lat_count - 1):
            pairs = first_pairs if lat % 2 else second_pairs
            pairs.append((device(lat, lon), device(lat + 1, lon)))
            pairs.append((device(lat + 1, lon), device(lat, lon)))
        first_pairs.append(
            (device(lat_count - 1, lon), device(lat_count - 1, lon_count - 1 - lon))
        )
    first_got = lax.ppermute(first_lines, ("lon", "lat"), first_pairs)
    second_got = lax.ppermute(second_lines, ("lon", "lat"), second_pairs)
    field = jax.ShapeDtypeStruct(potential_warmth.shape, jnp.float32)
    return pl.pallas_call(
        stencil_kernel,
        out_shape=(field, field),
        in_specs=[pl.BlockSpec(memory_space=vmem)] * 11,
        out_specs=(pl.BlockSpec(memory_space=vmem), pl.BlockSpec(memory_space=vmem)),
        scratch_shapes=[
            pltpu.VMEM((4, layer_total, rows, cols), jnp.float32),
            pltpu.VMEM((4, layer_total, rows, cols), jnp.float32),
            pltpu.VMEM((2, layer_total, rows, cols), jnp.float32),
            pltpu.VMEM((2, layer_total, rows, cols), jnp.float32),
            pltpu.VMEM((5, rows, cols), jnp.float32),
        ],
    )(
        potential_warmth,
        saltiness_anomaly,
        zonal_speed,
        meridional_speed,
        sinking_speed,
        water_indicator,
        seabed_layer_index,
        west_cols,
        east_cols,
        first_got,
        second_got,
    )


def solution(mesh):
    placed = (
        P(None, "lat", "lon"),
        P(None, "lat", "lon"),
        P(None, "lat", "lon"),
        P(None, "lat", "lon"),
        P(None, "lat", "lon"),
        P("lat", "lon"),
        P("lat", "lon"),
    )
    return jax.shard_map(
        on_device,
        mesh=mesh,
        in_specs=placed,
        out_specs=(P(None, "lat", "lon"), P(None, "lat", "lon")),
        check_vma=False,
    )
```

```python
import jax
import jax.numpy as jnp
from jax import lax
from jax.experimental import pallas as pl
from jax.experimental.pallas import tpu as pltpu
from jax.sharding import PartitionSpec as P

DIFFUSIVITY = 0.15
DENSITY_FLOOR = 0.5
SLOPE_LIMIT = 1.0
THERMAL = 0.25
HALINE = 0.75


def stencil_kernel(
    t_ref, s_ref, u_ref, v_ref, w_ref, wi_ref, sb_ref, hw_ref, he_ref,
    first_ref, second_ref, ot_ref, os_ref, tsh, ssh, ush, vsh, dsh,
):
    layer_total, rows, cols = t_ref.shape
    lane = lax.broadcasted_iota(jnp.int32, (rows, cols), 1)
    row = lax.broadcasted_iota(jnp.int32, (rows, cols), 0)
    east_edge = lane == cols - 1
    west_edge = lane == 0
    north_edge = row == rows - 1
    south_edge = row == 0

    def east_of(x, h):
        return jnp.where(east_edge, h, pltpu.roll(x, cols - 1, 1))

    def west_of(x, h):
        return jnp.where(west_edge, h, pltpu.roll(x, 1, 1))

    def north_of(x, h):
        return jnp.where(north_edge, h, pltpu.roll(x, rows - 1, 0))

    def south_of(x, h):
        return jnp.where(south_edge, h, pltpu.roll(x, 1, 0))

    lane_tile = hw_ref.shape[1]

    def column_of(ref, p, at):
        packed = ref[...]
        shift = (at - p) % lane_tile
        if shift:
            packed = pltpu.roll(packed, shift, 1)
        return jnp.concatenate([packed] * (cols // lane_tile), 1)

    def east_halo(p):
        return column_of(he_ref, p, lane_tile - 1)

    def west_halo(p):
        return column_of(hw_ref, p, 0)

    odd = lax.axis_index("lat") % 2 == 1

    def north_halo(p):
        return jnp.where(odd, first_ref[p : p + 1, :], second_ref[p : p + 1, :])

    def south_halo(p):
        return jnp.where(odd, second_ref[p : p + 1, :], first_ref[p : p + 1, :])

    depth_plane = 2 * layer_total
    depth = (wi_ref[...] * sb_ref[...]).astype(jnp.float32)
    dsh[0] = depth
    dsh[1] = east_of(depth, east_halo(depth_plane))
    dsh[2] = west_of(depth, west_halo(depth_plane))
    dsh[3] = north_of(depth, north_halo(depth_plane))
    dsh[4] = south_of(depth, south_halo(depth_plane))

    for k in range(layer_total):
        for src, dst, base in ((t_ref, tsh, 0), (s_ref, ssh, layer_total)):
            x = src[k]
            dst[0, k] = east_of(x, east_halo(base + k))
            dst[1, k] = west_of(x, west_halo(base + k))
            dst[2, k] = north_of(x, north_halo(base + k))
            dst[3, k] = south_of(x, south_halo(base + k))
        x = u_ref[k]
        ush[0, k] = east_of(x, east_halo(depth_plane + 1 + k))
        ush[1, k] = west_of(x, west_halo(depth_plane + 1 + k))
        x = v_ref[k]
        vsh[0, k] = north_of(x, north_halo(depth_plane + 1 + k))
        vsh[1, k] = south_of(x, south_halo(depth_plane + 1 + k))

    def planes(k):
        at = jnp.clip(k, 0, layer_total - 1)
        temp = [t_ref[at]] + [tsh[i, at] for i in range(4)]
        salt = [s_ref[at]] + [ssh[i, at] for i in range(4)]
        rho = [HALINE * sv - THERMAL * tv for tv, sv in zip(temp, salt)]
        return temp, salt, rho

    def wet_at(k):
        inside = jnp.logical_and(k >= 0, k < layer_total)
        level = k.astype(jnp.float32)
        return [
            jnp.where(jnp.logical_and(inside, level < dsh[i]), 1.0, 0.0) for i in range(5)
        ]

    sub_tile = 8

    def whole(x):
        return x

    def west_part(x):
        return x[:, :lane_tile]

    def south_part(x):
        return x[:sub_tile, :]

    def horizontal(fields, kcs, wet, a, b, speed_a, speed_b, part):
        face = part(wet[a]) * part(wet[b])
        temp, salt, rho = fields
        k_temp, k_salt, k_rho = kcs
        slope = jnp.clip(
            -((part(rho[b]) - part(rho[a])) * face)
            / jnp.maximum(0.5 * (k_rho[a] + k_rho[b]), DENSITY_FLOOR),
            -SLOPE_LIMIT,
            SLOPE_LIMIT,
        )
        flow = 0.5 * (part(speed_a) + part(speed_b)) * face
        up, down = jnp.maximum(flow, 0.0), jnp.minimum(flow, 0.0)
        out = []
        for x, kx in ((temp, k_temp), (salt, k_salt)):
            xa, xb = part(x[a]), part(x[b])
            grad = (xb - xa) * face
            out.append(
                up * xa + down * xb
                - DIFFUSIVITY * face * (grad + slope * (0.5 * (kx[a] + kx[b])))
            )
        return out

    def cell_means(x, wet):
        east_grad = (x[1] - x[0]) * (wet[0] * wet[1])
        west_grad = (x[0] - x[2]) * (wet[2] * wet[0])
        north_grad = (x[3] - x[0]) * (wet[0] * wet[3])
        south_grad = (x[0] - x[4]) * (wet[4] * wet[0])
        return 0.5 * (west_grad + east_grad), 0.5 * (south_grad + north_grad)

    def vertical_mean(lo, h, up, face_top, face_bottom, i, part):
        return 0.5 * (
            (part(h[i]) - part(lo[i])) * part(face_top[i])
            + (part(up[i]) - part(h[i])) * part(face_bottom[i])
        )

    def level_step(k, carry):
        down_temp, down_salt = carry[:2]
        means_here = [carry[2 + 2 * n : 4 + 2 * n] for n in range(3)]
        lower = planes(k - 1)
        here = planes(k)
        upper = planes(k + 1)
        wet_lower = wet_at(k - 1)
        wet_here = wet_at(k)
        wet_upper = wet_at(k + 1)
        face_top = [wet_here[i] * wet_lower[i] for i in range(5)]
        face_bottom = [wet_upper[i] * wet_here[i] for i in range(5)]

        def kc_set(i, part):
            return [
                vertical_mean(lo, h, up, face_top, face_bottom, i, part)
                for lo, h, up in zip(lower, here, upper)
            ]

        kc_full = [kc_set(i, whole) for i in (0, 1, 3)]
        kcs = [[kc_full[0][n], kc_full[1][n], None, kc_full[2][n], None] for n in range(3)]
        west_kcs = [[kc_set(0, west_part)[n], None, kc_set(2, west_part)[n], None, None] for n in range(3)]
        south_kcs = [[kc_set(0, south_part)[n], None, None, None, kc_set(4, south_part)[n]] for n in range(3)]
        zonal = u_ref[k]
        meridional = v_ref[k]
        east = horizontal(here, kcs, wet_here, 0, 1, zonal, ush[0, k], whole)
        west_edge_flux = horizontal(here, west_kcs, wet_here, 2, 0, ush[1, k], zonal, west_part)
        north = horizontal(here, kcs, wet_here, 0, 3, meridional, vsh[0, k], whole)
        south_edge_flux = horizontal(
            here, south_kcs, wet_here, 4, 0, vsh[1, k], meridional, south_part
        )
        west = [
            jnp.where(
                west_edge,
                jnp.concatenate([w] * (cols // lane_tile), 1),
                pltpu.roll(f, 1, 1),
            )
            for w, f in zip(west_edge_flux, east)
        ]
        south = [
            jnp.where(
                south_edge,
                jnp.concatenate([s] * (rows // sub_tile), 0),
                pltpu.roll(f, 1, 0),
            )
            for s, f in zip(south_edge_flux, north)
        ]
        means_upper = [cell_means(f, wet_upper) for f in upper]
        face = face_bottom[0]
        xu = [0.5 * (mh[0] + mu[0]) for mh, mu in zip(means_here, means_upper)]
        yu = [0.5 * (mh[1] + mu[1]) for mh, mu in zip(means_here, means_upper)]
        dk = [(up[0] - h[0]) * face for h, up in zip(here, upper)]
        floor = jnp.maximum(dk[2], DENSITY_FLOOR)
        slope_x = jnp.clip(-xu[2] / floor, -SLOPE_LIMIT, SLOPE_LIMIT)
        slope_y = jnp.clip(-yu[2] / floor, -SLOPE_LIMIT, SLOPE_LIMIT)
        above = jnp.clip(k + 1, 0, layer_total - 1)
        flow = 0.5 * (w_ref[k] + w_ref[above]) * face
        up, down = jnp.maximum(flow, 0.0), jnp.minimum(flow, 0.0)
        squares = slope_x * slope_x + slope_y * slope_y
        below = []
        for n in range(2):
            below.append(
                up * here[n][0] + down * upper[n][0]
                - DIFFUSIVITY * face * (slope_x * xu[n] + slope_y * yu[n] + squares * dk[n])
            )
        for n, (dst, top) in enumerate(((ot_ref, down_temp), (os_ref, down_salt))):
            divergence = (east[n] - west[n]) + (north[n] - south[n])
            divergence = divergence + (below[n] - top)
            dst[k] = here[n][0] - divergence
        return tuple(below) + tuple(m for pair in means_upper for m in pair)

    zero = jnp.zeros((rows, cols), jnp.float32)
    first_wet = wet_at(jnp.int32(0))
    first_means = [cell_means(f, first_wet) for f in planes(jnp.int32(0))]
    lax.fori_loop(
        0,
        layer_total,
        level_step,
        (zero, zero) + tuple(m for pair in first_means for m in pair),
    )


def edge_kernel(
    t_ref, s_ref, u_ref, v_ref, wi_ref, sb_ref,
    west_ref, east_ref, first_ref, second_ref, tops_ref, bottoms_ref,
):
    layer_total, rows, cols = t_ref.shape
    lane_tile = west_ref.shape[1]
    lat_index = lax.axis_index("lat")
    odd = lat_index % 2 == 1
    top = lat_index == lax.axis_size("lat") - 1
    depth = (wi_ref[...] * sb_ref[...]).astype(jnp.float32)
    lane = lax.broadcasted_iota(jnp.int32, (rows, lane_tile), 1)
    column_planes = (
        [t_ref[k] for k in range(layer_total)]
        + [s_ref[k] for k in range(layer_total)]
        + [depth]
        + [u_ref[k] for k in range(layer_total)]
    )
    west = jnp.zeros((rows, lane_tile), jnp.float32)
    east = jnp.zeros((rows, lane_tile), jnp.float32)
    for p, x in enumerate(column_planes):
        west = jnp.where(lane == p, x[:, cols - 1 :], west)
        east = jnp.where(lane == p, x[:, :1], east)
    west_ref[...] = west
    east_ref[...] = east
    base_planes = 2 * layer_total + 1
    row_planes = column_planes[:base_planes] + [v_ref[k] for k in range(layer_total)]
    for p, x in enumerate(row_planes):
        tops_ref[p : p + 1, :] = x[rows - 1 :, :]
        bottoms_ref[p : p + 1, :] = x[:1, :]
    tops = tops_ref[...]
    bottoms = bottoms_ref[...]
    line_lane = lax.broadcasted_iota(jnp.int32, tops.shape, 1)
    mirrored = tops
    step = 1
    while step < cols:
        mirrored = jnp.where(
            (line_lane & step) != 0,
            pltpu.roll(mirrored, step, 1),
            pltpu.roll(mirrored, cols - step, 1),
        )
        step *= 2
    plane = lax.broadcasted_iota(jnp.int32, tops.shape, 0)
    folded = jnp.where(plane >= base_planes, -mirrored, mirrored)
    first_ref[...] = jnp.where(top, folded, jnp.where(odd, tops, bottoms))
    second_ref[...] = jnp.where(odd, bottoms, tops)


def on_device(
    potential_warmth,
    saltiness_anomaly,
    zonal_speed,
    meridional_speed,
    sinking_speed,
    water_indicator,
    seabed_layer_index,
):
    layer_total, rows, cols = potential_warmth.shape
    base_planes = 2 * layer_total + 1
    halo_planes = 3 * layer_total + 1
    lane_tile = 128
    lon_count = lax.axis_size("lon")
    lat_count = lax.axis_size("lat")
    lat_index = lax.axis_index("lat")
    odd = lat_index % 2
    vmem = pltpu.MemorySpace.VMEM
    smem = pltpu.MemorySpace.SMEM
    packed = jax.ShapeDtypeStruct((rows, lane_tile), jnp.float32)
    lines = jax.ShapeDtypeStruct((halo_planes, cols), jnp.float32)
    west_pack, east_pack, first_lines, second_lines = pl.pallas_call(
        edge_kernel,
        out_shape=(packed, packed, lines, lines),
        in_specs=[pl.BlockSpec(memory_space=vmem)] * 6,
        out_specs=tuple(pl.BlockSpec(memory_space=vmem) for _ in range(4)),
        scratch_shapes=[
            pltpu.VMEM((halo_planes, cols), jnp.float32),
            pltpu.VMEM((halo_planes, cols), jnp.float32),
        ],
    )(
        potential_warmth,
        saltiness_anomaly,
        zonal_speed,
        meridional_speed,
        water_indicator,
        seabed_layer_index,
    )

    west_cols = lax.ppermute(
        west_pack, "lon", [(i, (i + 1) % lon_count) for i in range(lon_count)]
    )
    east_cols = lax.ppermute(
        east_pack, "lon", [((i + 1) % lon_count, i) for i in range(lon_count)]
    )

    def device(lat, lon):
        return lon * lat_count + lat

    first_pairs = []
    second_pairs = []
    for lon in range(lon_count):
        for lat in range(lat_count - 1):
            pairs = first_pairs if lat % 2 else second_pairs
            pairs.append((device(lat, lon), device(lat + 1, lon)))
            pairs.append((device(lat + 1, lon), device(lat, lon)))
        first_pairs.append(
            (device(lat_count - 1, lon), device(lat_count - 1, lon_count - 1 - lon))
        )
    first_got = lax.ppermute(first_lines, ("lon", "lat"), first_pairs)
    second_got = lax.ppermute(second_lines, ("lon", "lat"), second_pairs)
    field = jax.ShapeDtypeStruct(potential_warmth.shape, jnp.float32)
    return pl.pallas_call(
        stencil_kernel,
        out_shape=(field, field),
        in_specs=[pl.BlockSpec(memory_space=vmem)] * 11,
        out_specs=(pl.BlockSpec(memory_space=vmem), pl.BlockSpec(memory_space=vmem)),
        scratch_shapes=[
            pltpu.VMEM((4, layer_total, rows, cols), jnp.float32),
            pltpu.VMEM((4, layer_total, rows, cols), jnp.float32),
            pltpu.VMEM((2, layer_total, rows, cols), jnp.float32),
            pltpu.VMEM((2, layer_total, rows, cols), jnp.float32),
            pltpu.VMEM((5, rows, cols), jnp.float32),
        ],
    )(
        potential_warmth,
        saltiness_anomaly,
        zonal_speed,
        meridional_speed,
        sinking_speed,
        water_indicator,
        seabed_layer_index,
        west_cols,
        east_cols,
        first_got,
        second_got,
    )


def solution(mesh):
    placed = (
        P(None, "lat", "lon"),
        P(None, "lat", "lon"),
        P(None, "lat", "lon"),
        P(None, "lat", "lon"),
        P(None, "lat", "lon"),
        P("lat", "lon"),
        P("lat", "lon"),
    )
    return jax.shard_map(
        on_device,
        mesh=mesh,
        in_specs=placed,
        out_specs=(P(None, "lat", "lon"), P(None, "lat", "lon")),
        check_vma=False,
    )
```

```python
import jax
import jax.numpy as jnp
from jax import lax
from jax.experimental import pallas as pl
from jax.experimental.pallas import tpu as pltpu
from jax.sharding import PartitionSpec as P

DIFFUSIVITY = 0.15
DENSITY_FLOOR = 0.5
SLOPE_LIMIT = 1.0
THERMAL = 0.25
HALINE = 0.75


def stencil_kernel(
    t_ref, s_ref, u_ref, v_ref, w_ref, wi_ref, sb_ref, hw_ref, he_ref,
    first_ref, second_ref, ot_ref, os_ref, tsh, ssh, ush, vsh, dsh,
):
    layer_total, rows, cols = t_ref.shape
    lane = lax.broadcasted_iota(jnp.int32, (rows, cols), 1)
    row = lax.broadcasted_iota(jnp.int32, (rows, cols), 0)
    east_edge = lane == cols - 1
    west_edge = lane == 0
    north_edge = row == rows - 1
    south_edge = row == 0

    def east_of(x, h):
        return jnp.where(east_edge, h, pltpu.roll(x, cols - 1, 1))

    def west_of(x, h):
        return jnp.where(west_edge, h, pltpu.roll(x, 1, 1))

    def north_of(x, h):
        return jnp.where(north_edge, h, pltpu.roll(x, rows - 1, 0))

    def south_of(x, h):
        return jnp.where(south_edge, h, pltpu.roll(x, 1, 0))

    lane_tile = hw_ref.shape[1]

    def column_of(ref, p, at):
        packed = ref[...]
        shift = (at - p) % lane_tile
        if shift:
            packed = pltpu.roll(packed, shift, 1)
        return jnp.concatenate([packed] * (cols // lane_tile), 1)

    def east_halo(p):
        return column_of(he_ref, p, lane_tile - 1)

    def west_halo(p):
        return column_of(hw_ref, p, 0)

    odd = lax.axis_index("lat") % 2 == 1

    def north_halo(p):
        return jnp.where(odd, first_ref[p : p + 1, :], second_ref[p : p + 1, :])

    def south_halo(p):
        return jnp.where(odd, second_ref[p : p + 1, :], first_ref[p : p + 1, :])

    depth_plane = 2 * layer_total
    depth = (wi_ref[...] * sb_ref[...]).astype(jnp.float32)
    dsh[0] = depth
    dsh[1] = east_of(depth, east_halo(depth_plane))
    dsh[2] = west_of(depth, west_halo(depth_plane))
    dsh[3] = north_of(depth, north_halo(depth_plane))
    dsh[4] = south_of(depth, south_halo(depth_plane))

    for k in range(layer_total):
        for src, dst, base in ((t_ref, tsh, 0), (s_ref, ssh, layer_total)):
            x = src[k]
            dst[0, k] = east_of(x, east_halo(base + k))
            dst[1, k] = west_of(x, west_halo(base + k))
            dst[2, k] = north_of(x, north_halo(base + k))
            dst[3, k] = south_of(x, south_halo(base + k))
        x = u_ref[k]
        ush[0, k] = east_of(x, east_halo(depth_plane + 1 + k))
        ush[1, k] = west_of(x, west_halo(depth_plane + 1 + k))
        x = v_ref[k]
        vsh[0, k] = north_of(x, north_halo(depth_plane + 1 + k))
        vsh[1, k] = south_of(x, south_halo(depth_plane + 1 + k))

    def planes(k):
        at = jnp.clip(k, 0, layer_total - 1)
        temp = [t_ref[at]] + [tsh[i, at] for i in range(4)]
        salt = [s_ref[at]] + [ssh[i, at] for i in range(4)]
        rho = [HALINE * sv - THERMAL * tv for tv, sv in zip(temp, salt)]
        return temp, salt, rho

    def wet_at(k):
        inside = jnp.logical_and(k >= 0, k < layer_total)
        level = k.astype(jnp.float32)
        return [
            jnp.where(jnp.logical_and(inside, level < dsh[i]), 1.0, 0.0) for i in range(5)
        ]

    sub_tile = 8

    def whole(x):
        return x

    def west_part(x):
        return x[:, :lane_tile]

    def south_part(x):
        return x[:sub_tile, :]

    def horizontal(fields, kcs, wet, a, b, speed_a, speed_b, part):
        face = part(wet[a]) * part(wet[b])
        temp, salt, rho = fields
        k_temp, k_salt, k_rho = kcs
        slope = jnp.clip(
            -((part(rho[b]) - part(rho[a])) * face)
            / jnp.maximum(0.5 * (k_rho[a] + k_rho[b]), DENSITY_FLOOR),
            -SLOPE_LIMIT,
            SLOPE_LIMIT,
        )
        flow = 0.5 * (part(speed_a) + part(speed_b)) * face
        up, down = jnp.maximum(flow, 0.0), jnp.minimum(flow, 0.0)
        out = []
        for x, kx in ((temp, k_temp), (salt, k_salt)):
            xa, xb = part(x[a]), part(x[b])
            grad = (xb - xa) * face
            out.append(
                up * xa + down * xb
                - DIFFUSIVITY * face * (grad + slope * (0.5 * (kx[a] + kx[b])))
            )
        return out

    def cell_means(x, wet):
        east_grad = (x[1] - x[0]) * (wet[0] * wet[1])
        west_grad = (x[0] - x[2]) * (wet[2] * wet[0])
        north_grad = (x[3] - x[0]) * (wet[0] * wet[3])
        south_grad = (x[0] - x[4]) * (wet[4] * wet[0])
        return 0.5 * (west_grad + east_grad), 0.5 * (south_grad + north_grad)

    def vertical_mean(lo, h, up, face_top, face_bottom, i, part):
        return 0.5 * (
            (part(h[i]) - part(lo[i])) * part(face_top[i])
            + (part(up[i]) - part(h[i])) * part(face_bottom[i])
        )

    def level_step(k, carry):
        down_temp, down_salt = carry[:2]
        means_here = [carry[2 + 2 * n : 4 + 2 * n] for n in range(3)]
        face_top = list(carry[8:13])
        lower = planes(k - 1)
        here = planes(k)
        upper = planes(k + 1)
        wet_here = wet_at(k)
        wet_upper = wet_at(k + 1)
        face_bottom = [wet_upper[i] * wet_here[i] for i in range(5)]

        def kc_set(i, part):
            return [
                vertical_mean(lo, h, up, face_top, face_bottom, i, part)
                for lo, h, up in zip(lower, here, upper)
            ]

        kc_full = [kc_set(i, whole) for i in (0, 1, 3)]
        kcs = [[kc_full[0][n], kc_full[1][n], None, kc_full[2][n], None] for n in range(3)]
        west_kcs = [[kc_set(0, west_part)[n], None, kc_set(2, west_part)[n], None, None] for n in range(3)]
        south_kcs = [[kc_set(0, south_part)[n], None, None, None, kc_set(4, south_part)[n]] for n in range(3)]
        zonal = u_ref[k]
        meridional = v_ref[k]
        east = horizontal(here, kcs, wet_here, 0, 1, zonal, ush[0, k], whole)
        west_edge_flux = horizontal(here, west_kcs, wet_here, 2, 0, ush[1, k], zonal, west_part)
        north = horizontal(here, kcs, wet_here, 0, 3, meridional, vsh[0, k], whole)
        south_edge_flux = horizontal(
            here, south_kcs, wet_here, 4, 0, vsh[1, k], meridional, south_part
        )
        west = [
            jnp.where(
                west_edge,
                jnp.concatenate([w] * (cols // lane_tile), 1),
                pltpu.roll(f, 1, 1),
            )
            for w, f in zip(west_edge_flux, east)
        ]
        south = [
            jnp.where(
                south_edge,
                jnp.concatenate([s] * (rows // sub_tile), 0),
                pltpu.roll(f, 1, 0),
            )
            for s, f in zip(south_edge_flux, north)
        ]
        means_upper = [cell_means(f, wet_upper) for f in upper]
        face = face_bottom[0]
        xu = [0.5 * (mh[0] + mu[0]) for mh, mu in zip(means_here, means_upper)]
        yu = [0.5 * (mh[1] + mu[1]) for mh, mu in zip(means_here, means_upper)]
        dk = [(up[0] - h[0]) * face for h, up in zip(here, upper)]
        floor = jnp.maximum(dk[2], DENSITY_FLOOR)
        slope_x = jnp.clip(-xu[2] / floor, -SLOPE_LIMIT, SLOPE_LIMIT)
        slope_y = jnp.clip(-yu[2] / floor, -SLOPE_LIMIT, SLOPE_LIMIT)
        above = jnp.clip(k + 1, 0, layer_total - 1)
        flow = 0.5 * (w_ref[k] + w_ref[above]) * face
        up, down = jnp.maximum(flow, 0.0), jnp.minimum(flow, 0.0)
        squares = slope_x * slope_x + slope_y * slope_y
        below = []
        for n in range(2):
            below.append(
                up * here[n][0] + down * upper[n][0]
                - DIFFUSIVITY * face * (slope_x * xu[n] + slope_y * yu[n] + squares * dk[n])
            )
        for n, (dst, top) in enumerate(((ot_ref, down_temp), (os_ref, down_salt))):
            divergence = (east[n] - west[n]) + (north[n] - south[n])
            divergence = divergence + (below[n] - top)
            dst[k] = here[n][0] - divergence
        return (
            tuple(below) + tuple(m for pair in means_upper for m in pair) + tuple(face_bottom)
        )

    zero = jnp.zeros((rows, cols), jnp.float32)
    first_wet = wet_at(jnp.int32(0))
    first_means = [cell_means(f, first_wet) for f in planes(jnp.int32(0))]
    lax.fori_loop(
        0,
        layer_total,
        level_step,
        (zero, zero) + tuple(m for pair in first_means for m in pair) + (zero,) * 5,
    )


def edge_kernel(
    t_ref, s_ref, u_ref, v_ref, wi_ref, sb_ref,
    west_ref, east_ref, first_ref, second_ref, tops_ref, bottoms_ref,
):
    layer_total, rows, cols = t_ref.shape
    lane_tile = west_ref.shape[1]
    lat_index = lax.axis_index("lat")
    odd = lat_index % 2 == 1
    top = lat_index == lax.axis_size("lat") - 1
    depth = (wi_ref[...] * sb_ref[...]).astype(jnp.float32)
    lane = lax.broadcasted_iota(jnp.int32, (rows, lane_tile), 1)
    column_planes = (
        [t_ref[k] for k in range(layer_total)]
        + [s_ref[k] for k in range(layer_total)]
        + [depth]
        + [u_ref[k] for k in range(layer_total)]
    )
    west = jnp.zeros((rows, lane_tile), jnp.float32)
    east = jnp.zeros((rows, lane_tile), jnp.float32)
    for p, x in enumerate(column_planes):
        west = jnp.where(lane == p, x[:, cols - 1 :], west)
        east = jnp.where(lane == p, x[:, :1], east)
    west_ref[...] = west
    east_ref[...] = east
    base_planes = 2 * layer_total + 1
    row_planes = column_planes[:base_planes] + [v_ref[k] for k in range(layer_total)]
    for p, x in enumerate(row_planes):
        tops_ref[p : p + 1, :] = x[rows - 1 :, :]
        bottoms_ref[p : p + 1, :] = x[:1, :]
    tops = tops_ref[...]
    bottoms = bottoms_ref[...]
    line_lane = lax.broadcasted_iota(jnp.int32, tops.shape, 1)
    mirrored = tops
    step = 1
    while step < cols:
        mirrored = jnp.where(
            (line_lane & step) != 0,
            pltpu.roll(mirrored, step, 1),
            pltpu.roll(mirrored, cols - step, 1),
        )
        step *= 2
    plane = lax.broadcasted_iota(jnp.int32, tops.shape, 0)
    folded = jnp.where(plane >= base_planes, -mirrored, mirrored)
    first_ref[...] = jnp.where(top, folded, jnp.where(odd, tops, bottoms))
    second_ref[...] = jnp.where(odd, bottoms, tops)


def on_device(
    potential_warmth,
    saltiness_anomaly,
    zonal_speed,
    meridional_speed,
    sinking_speed,
    water_indicator,
    seabed_layer_index,
):
    layer_total, rows, cols = potential_warmth.shape
    base_planes = 2 * layer_total + 1
    halo_planes = 3 * layer_total + 1
    lane_tile = 128
    lon_count = lax.axis_size("lon")
    lat_count = lax.axis_size("lat")
    lat_index = lax.axis_index("lat")
    odd = lat_index % 2
    vmem = pltpu.MemorySpace.VMEM
    smem = pltpu.MemorySpace.SMEM
    packed = jax.ShapeDtypeStruct((rows, lane_tile), jnp.float32)
    lines = jax.ShapeDtypeStruct((halo_planes, cols), jnp.float32)
    west_pack, east_pack, first_lines, second_lines = pl.pallas_call(
        edge_kernel,
        out_shape=(packed, packed, lines, lines),
        in_specs=[pl.BlockSpec(memory_space=vmem)] * 6,
        out_specs=tuple(pl.BlockSpec(memory_space=vmem) for _ in range(4)),
        scratch_shapes=[
            pltpu.VMEM((halo_planes, cols), jnp.float32),
            pltpu.VMEM((halo_planes, cols), jnp.float32),
        ],
    )(
        potential_warmth,
        saltiness_anomaly,
        zonal_speed,
        meridional_speed,
        water_indicator,
        seabed_layer_index,
    )

    west_cols = lax.ppermute(
        west_pack, "lon", [(i, (i + 1) % lon_count) for i in range(lon_count)]
    )
    east_cols = lax.ppermute(
        east_pack, "lon", [((i + 1) % lon_count, i) for i in range(lon_count)]
    )

    def device(lat, lon):
        return lon * lat_count + lat

    first_pairs = []
    second_pairs = []
    for lon in range(lon_count):
        for lat in range(lat_count - 1):
            pairs = first_pairs if lat % 2 else second_pairs
            pairs.append((device(lat, lon), device(lat + 1, lon)))
            pairs.append((device(lat + 1, lon), device(lat, lon)))
        first_pairs.append(
            (device(lat_count - 1, lon), device(lat_count - 1, lon_count - 1 - lon))
        )
    first_got = lax.ppermute(first_lines, ("lon", "lat"), first_pairs)
    second_got = lax.ppermute(second_lines, ("lon", "lat"), second_pairs)
    field = jax.ShapeDtypeStruct(potential_warmth.shape, jnp.float32)
    return pl.pallas_call(
        stencil_kernel,
        out_shape=(field, field),
        in_specs=[pl.BlockSpec(memory_space=vmem)] * 11,
        out_specs=(pl.BlockSpec(memory_space=vmem), pl.BlockSpec(memory_space=vmem)),
        scratch_shapes=[
            pltpu.VMEM((4, layer_total, rows, cols), jnp.float32),
            pltpu.VMEM((4, layer_total, rows, cols), jnp.float32),
            pltpu.VMEM((2, layer_total, rows, cols), jnp.float32),
            pltpu.VMEM((2, layer_total, rows, cols), jnp.float32),
            pltpu.VMEM((5, rows, cols), jnp.float32),
        ],
    )(
        potential_warmth,
        saltiness_anomaly,
        zonal_speed,
        meridional_speed,
        sinking_speed,
        water_indicator,
        seabed_layer_index,
        west_cols,
        east_cols,
        first_got,
        second_got,
    )


def solution(mesh):
    placed = (
        P(None, "lat", "lon"),
        P(None, "lat", "lon"),
        P(None, "lat", "lon"),
        P(None, "lat", "lon"),
        P(None, "lat", "lon"),
        P("lat", "lon"),
        P("lat", "lon"),
    )
    return jax.shard_map(
        on_device,
        mesh=mesh,
        in_specs=placed,
        out_specs=(P(None, "lat", "lon"), P(None, "lat", "lon")),
        check_vma=False,
    )
```

```python
import jax
import jax.numpy as jnp
from jax import lax
from jax.experimental import pallas as pl
from jax.experimental.pallas import tpu as pltpu
from jax.sharding import PartitionSpec as P

DIFFUSIVITY = 0.15
DENSITY_FLOOR = 0.5
SLOPE_LIMIT = 1.0
THERMAL = 0.25
HALINE = 0.75


def stencil_kernel(
    t_ref, s_ref, u_ref, v_ref, w_ref, wi_ref, sb_ref, hw_ref, he_ref,
    first_ref, second_ref, ot_ref, os_ref, tsh, ssh, ush, vsh, dsh,
):
    layer_total, rows, cols = t_ref.shape
    lane = lax.broadcasted_iota(jnp.int32, (rows, cols), 1)
    row = lax.broadcasted_iota(jnp.int32, (rows, cols), 0)
    east_edge = lane == cols - 1
    west_edge = lane == 0
    north_edge = row == rows - 1
    south_edge = row == 0

    def east_of(x, h):
        return jnp.where(east_edge, h, pltpu.roll(x, cols - 1, 1))

    def west_of(x, h):
        return jnp.where(west_edge, h, pltpu.roll(x, 1, 1))

    def north_of(x, h):
        return jnp.where(north_edge, h, pltpu.roll(x, rows - 1, 0))

    def south_of(x, h):
        return jnp.where(south_edge, h, pltpu.roll(x, 1, 0))

    lane_tile = hw_ref.shape[1]

    def column_of(ref, p, at):
        packed = ref[...]
        shift = (at - p) % lane_tile
        if shift:
            packed = pltpu.roll(packed, shift, 1)
        return jnp.concatenate([packed] * (cols // lane_tile), 1)

    def east_halo(p):
        return column_of(he_ref, p, lane_tile - 1)

    def west_halo(p):
        return column_of(hw_ref, p, 0)

    odd = lax.axis_index("lat") % 2 == 1

    def north_halo(p):
        return jnp.where(odd, first_ref[p : p + 1, :], second_ref[p : p + 1, :])

    def south_halo(p):
        return jnp.where(odd, second_ref[p : p + 1, :], first_ref[p : p + 1, :])

    depth_plane = 2 * layer_total
    depth = (wi_ref[...] * sb_ref[...]).astype(jnp.float32)
    dsh[0] = depth
    dsh[1] = east_of(depth, east_halo(depth_plane))
    dsh[2] = west_of(depth, west_halo(depth_plane))
    dsh[3] = north_of(depth, north_halo(depth_plane))
    dsh[4] = south_of(depth, south_halo(depth_plane))

    for k in range(layer_total):
        for src, dst, base in ((t_ref, tsh, 0), (s_ref, ssh, layer_total)):
            x = src[k]
            dst[0, k] = east_of(x, east_halo(base + k))
            dst[1, k] = west_of(x, west_halo(base + k))
            dst[2, k] = north_of(x, north_halo(base + k))
            dst[3, k] = south_of(x, south_halo(base + k))
        x = u_ref[k]
        ush[0, k] = east_of(x, east_halo(depth_plane + 1 + k))
        ush[1, k] = west_of(x, west_halo(depth_plane + 1 + k))
        x = v_ref[k]
        vsh[0, k] = north_of(x, north_halo(depth_plane + 1 + k))
        vsh[1, k] = south_of(x, south_halo(depth_plane + 1 + k))

    def planes(k):
        at = jnp.clip(k, 0, layer_total - 1)
        temp = [t_ref[at]] + [tsh[i, at] for i in range(4)]
        salt = [s_ref[at]] + [ssh[i, at] for i in range(4)]
        rho = [HALINE * sv - THERMAL * tv for tv, sv in zip(temp, salt)]
        return temp, salt, rho

    def wet_at(k):
        inside = jnp.logical_and(k >= 0, k < layer_total)
        level = k.astype(jnp.float32)
        return [
            jnp.where(jnp.logical_and(inside, level < dsh[i]), 1.0, 0.0) for i in range(5)
        ]

    sub_tile = 8

    def whole(x):
        return x

    def west_part(x):
        return x[:, :lane_tile]

    def south_part(x):
        return x[:sub_tile, :]

    def horizontal(fields, kcs, wet, a, b, speed_a, speed_b, part):
        face = part(wet[a]) * part(wet[b])
        temp, salt, rho = fields
        k_temp, k_salt, k_rho = kcs
        slope = jnp.clip(
            -((part(rho[b]) - part(rho[a])) * face)
            / jnp.maximum(0.5 * (k_rho[a] + k_rho[b]), DENSITY_FLOOR),
            -SLOPE_LIMIT,
            SLOPE_LIMIT,
        )
        flow = 0.5 * (part(speed_a) + part(speed_b)) * face
        up, down = jnp.maximum(flow, 0.0), jnp.minimum(flow, 0.0)
        out = []
        for x, kx in ((temp, k_temp), (salt, k_salt)):
            xa, xb = part(x[a]), part(x[b])
            grad = (xb - xa) * face
            out.append(
                up * xa + down * xb
                - DIFFUSIVITY * face * (grad + slope * (0.5 * (kx[a] + kx[b])))
            )
        return out

    def cell_means(x, wet):
        east_grad = (x[1] - x[0]) * (wet[0] * wet[1])
        west_grad = (x[0] - x[2]) * (wet[2] * wet[0])
        north_grad = (x[3] - x[0]) * (wet[0] * wet[3])
        south_grad = (x[0] - x[4]) * (wet[4] * wet[0])
        return 0.5 * (west_grad + east_grad), 0.5 * (south_grad + north_grad)

    def vertical_mean(lo, h, up, face_top, face_bottom, i, part):
        return 0.5 * (
            (part(h[i]) - part(lo[i])) * part(face_top[i])
            + (part(up[i]) - part(h[i])) * part(face_bottom[i])
        )

    def level_step(k, carry):
        down_temp, down_salt = carry[:2]
        means_here = [carry[2 + 2 * n : 4 + 2 * n] for n in range(3)]
        face_top = list(carry[8:13])
        wet_here = list(carry[13:18])
        lower = planes(k - 1)
        here = planes(k)
        upper = planes(k + 1)
        wet_upper = wet_at(k + 1)
        face_bottom = [wet_upper[i] * wet_here[i] for i in range(5)]

        def kc_set(i, part):
            return [
                vertical_mean(lo, h, up, face_top, face_bottom, i, part)
                for lo, h, up in zip(lower, here, upper)
            ]

        kc_full = [kc_set(i, whole) for i in (0, 1, 3)]
        kcs = [[kc_full[0][n], kc_full[1][n], None, kc_full[2][n], None] for n in range(3)]
        west_kcs = [[kc_set(0, west_part)[n], None, kc_set(2, west_part)[n], None, None] for n in range(3)]
        south_kcs = [[kc_set(0, south_part)[n], None, None, None, kc_set(4, south_part)[n]] for n in range(3)]
        zonal = u_ref[k]
        meridional = v_ref[k]
        east = horizontal(here, kcs, wet_here, 0, 1, zonal, ush[0, k], whole)
        west_edge_flux = horizontal(here, west_kcs, wet_here, 2, 0, ush[1, k], zonal, west_part)
        north = horizontal(here, kcs, wet_here, 0, 3, meridional, vsh[0, k], whole)
        south_edge_flux = horizontal(
            here, south_kcs, wet_here, 4, 0, vsh[1, k], meridional, south_part
        )
        west = [
            jnp.where(
                west_edge,
                jnp.concatenate([w] * (cols // lane_tile), 1),
                pltpu.roll(f, 1, 1),
            )
            for w, f in zip(west_edge_flux, east)
        ]
        south = [
            jnp.where(
                south_edge,
                jnp.concatenate([s] * (rows // sub_tile), 0),
                pltpu.roll(f, 1, 0),
            )
            for s, f in zip(south_edge_flux, north)
        ]
        means_upper = [cell_means(f, wet_upper) for f in upper]
        face = face_bottom[0]
        xu = [0.5 * (mh[0] + mu[0]) for mh, mu in zip(means_here, means_upper)]
        yu = [0.5 * (mh[1] + mu[1]) for mh, mu in zip(means_here, means_upper)]
        dk = [(up[0] - h[0]) * face for h, up in zip(here, upper)]
        floor = jnp.maximum(dk[2], DENSITY_FLOOR)
        slope_x = jnp.clip(-xu[2] / floor, -SLOPE_LIMIT, SLOPE_LIMIT)
        slope_y = jnp.clip(-yu[2] / floor, -SLOPE_LIMIT, SLOPE_LIMIT)
        above = jnp.clip(k + 1, 0, layer_total - 1)
        flow = 0.5 * (w_ref[k] + w_ref[above]) * face
        up, down = jnp.maximum(flow, 0.0), jnp.minimum(flow, 0.0)
        squares = slope_x * slope_x + slope_y * slope_y
        below = []
        for n in range(2):
            below.append(
                up * here[n][0] + down * upper[n][0]
                - DIFFUSIVITY * face * (slope_x * xu[n] + slope_y * yu[n] + squares * dk[n])
            )
        for n, (dst, top) in enumerate(((ot_ref, down_temp), (os_ref, down_salt))):
            divergence = (east[n] - west[n]) + (north[n] - south[n])
            divergence = divergence + (below[n] - top)
            dst[k] = here[n][0] - divergence
        return (
            tuple(below)
            + tuple(m for pair in means_upper for m in pair)
            + tuple(face_bottom)
            + tuple(wet_upper)
        )

    zero = jnp.zeros((rows, cols), jnp.float32)
    first_wet = wet_at(jnp.int32(0))
    first_means = [cell_means(f, first_wet) for f in planes(jnp.int32(0))]
    lax.fori_loop(
        0,
        layer_total,
        level_step,
        (zero, zero)
        + tuple(m for pair in first_means for m in pair)
        + (zero,) * 5
        + tuple(first_wet),
    )


def edge_kernel(
    t_ref, s_ref, u_ref, v_ref, wi_ref, sb_ref,
    west_ref, east_ref, first_ref, second_ref, tops_ref, bottoms_ref,
):
    layer_total, rows, cols = t_ref.shape
    lane_tile = west_ref.shape[1]
    lat_index = lax.axis_index("lat")
    odd = lat_index % 2 == 1
    top = lat_index == lax.axis_size("lat") - 1
    depth = (wi_ref[...] * sb_ref[...]).astype(jnp.float32)
    lane = lax.broadcasted_iota(jnp.int32, (rows, lane_tile), 1)
    column_planes = (
        [t_ref[k] for k in range(layer_total)]
        + [s_ref[k] for k in range(layer_total)]
        + [depth]
        + [u_ref[k] for k in range(layer_total)]
    )
    west = jnp.zeros((rows, lane_tile), jnp.float32)
    east = jnp.zeros((rows, lane_tile), jnp.float32)
    for p, x in enumerate(column_planes):
        west = jnp.where(lane == p, x[:, cols - 1 :], west)
        east = jnp.where(lane == p, x[:, :1], east)
    west_ref[...] = west
    east_ref[...] = east
    base_planes = 2 * layer_total + 1
    row_planes = column_planes[:base_planes] + [v_ref[k] for k in range(layer_total)]
    for p, x in enumerate(row_planes):
        tops_ref[p : p + 1, :] = x[rows - 1 :, :]
        bottoms_ref[p : p + 1, :] = x[:1, :]
    tops = tops_ref[...]
    bottoms = bottoms_ref[...]
    line_lane = lax.broadcasted_iota(jnp.int32, tops.shape, 1)
    mirrored = tops
    step = 1
    while step < cols:
        mirrored = jnp.where(
            (line_lane & step) != 0,
            pltpu.roll(mirrored, step, 1),
            pltpu.roll(mirrored, cols - step, 1),
        )
        step *= 2
    plane = lax.broadcasted_iota(jnp.int32, tops.shape, 0)
    folded = jnp.where(plane >= base_planes, -mirrored, mirrored)
    first_ref[...] = jnp.where(top, folded, jnp.where(odd, tops, bottoms))
    second_ref[...] = jnp.where(odd, bottoms, tops)


def on_device(
    potential_warmth,
    saltiness_anomaly,
    zonal_speed,
    meridional_speed,
    sinking_speed,
    water_indicator,
    seabed_layer_index,
):
    layer_total, rows, cols = potential_warmth.shape
    base_planes = 2 * layer_total + 1
    halo_planes = 3 * layer_total + 1
    lane_tile = 128
    lon_count = lax.axis_size("lon")
    lat_count = lax.axis_size("lat")
    lat_index = lax.axis_index("lat")
    odd = lat_index % 2
    vmem = pltpu.MemorySpace.VMEM
    smem = pltpu.MemorySpace.SMEM
    packed = jax.ShapeDtypeStruct((rows, lane_tile), jnp.float32)
    lines = jax.ShapeDtypeStruct((halo_planes, cols), jnp.float32)
    west_pack, east_pack, first_lines, second_lines = pl.pallas_call(
        edge_kernel,
        out_shape=(packed, packed, lines, lines),
        in_specs=[pl.BlockSpec(memory_space=vmem)] * 6,
        out_specs=tuple(pl.BlockSpec(memory_space=vmem) for _ in range(4)),
        scratch_shapes=[
            pltpu.VMEM((halo_planes, cols), jnp.float32),
            pltpu.VMEM((halo_planes, cols), jnp.float32),
        ],
    )(
        potential_warmth,
        saltiness_anomaly,
        zonal_speed,
        meridional_speed,
        water_indicator,
        seabed_layer_index,
    )

    west_cols = lax.ppermute(
        west_pack, "lon", [(i, (i + 1) % lon_count) for i in range(lon_count)]
    )
    east_cols = lax.ppermute(
        east_pack, "lon", [((i + 1) % lon_count, i) for i in range(lon_count)]
    )

    def device(lat, lon):
        return lon * lat_count + lat

    first_pairs = []
    second_pairs = []
    for lon in range(lon_count):
        for lat in range(lat_count - 1):
            pairs = first_pairs if lat % 2 else second_pairs
            pairs.append((device(lat, lon), device(lat + 1, lon)))
            pairs.append((device(lat + 1, lon), device(lat, lon)))
        first_pairs.append(
            (device(lat_count - 1, lon), device(lat_count - 1, lon_count - 1 - lon))
        )
    first_got = lax.ppermute(first_lines, ("lon", "lat"), first_pairs)
    second_got = lax.ppermute(second_lines, ("lon", "lat"), second_pairs)
    field = jax.ShapeDtypeStruct(potential_warmth.shape, jnp.float32)
    return pl.pallas_call(
        stencil_kernel,
        out_shape=(field, field),
        in_specs=[pl.BlockSpec(memory_space=vmem)] * 11,
        out_specs=(pl.BlockSpec(memory_space=vmem), pl.BlockSpec(memory_space=vmem)),
        scratch_shapes=[
            pltpu.VMEM((4, layer_total, rows, cols), jnp.float32),
            pltpu.VMEM((4, layer_total, rows, cols), jnp.float32),
            pltpu.VMEM((2, layer_total, rows, cols), jnp.float32),
            pltpu.VMEM((2, layer_total, rows, cols), jnp.float32),
            pltpu.VMEM((5, rows, cols), jnp.float32),
        ],
    )(
        potential_warmth,
        saltiness_anomaly,
        zonal_speed,
        meridional_speed,
        sinking_speed,
        water_indicator,
        seabed_layer_index,
        west_cols,
        east_cols,
        first_got,
        second_got,
    )


def solution(mesh):
    placed = (
        P(None, "lat", "lon"),
        P(None, "lat", "lon"),
        P(None, "lat", "lon"),
        P(None, "lat", "lon"),
        P(None, "lat", "lon"),
        P("lat", "lon"),
        P("lat", "lon"),
    )
    return jax.shard_map(
        on_device,
        mesh=mesh,
        in_specs=placed,
        out_specs=(P(None, "lat", "lon"), P(None, "lat", "lon")),
        check_vma=False,
    )
```

```python
import jax
import jax.numpy as jnp
from jax import lax
from jax.experimental import pallas as pl
from jax.experimental.pallas import tpu as pltpu
from jax.sharding import PartitionSpec as P

DIFFUSIVITY = 0.15
DENSITY_FLOOR = 0.5
SLOPE_LIMIT = 1.0
THERMAL = 0.25
HALINE = 0.75


def stencil_kernel(
    t_ref, s_ref, u_ref, v_ref, w_ref, wi_ref, sb_ref, hw_ref, he_ref,
    first_ref, second_ref, ot_ref, os_ref, tsh, ssh, ush, vsh, dsh,
):
    layer_total, rows, cols = t_ref.shape
    lane = lax.broadcasted_iota(jnp.int32, (rows, cols), 1)
    row = lax.broadcasted_iota(jnp.int32, (rows, cols), 0)
    east_edge = lane == cols - 1
    west_edge = lane == 0
    north_edge = row == rows - 1
    south_edge = row == 0

    def east_of(x, h):
        return jnp.where(east_edge, h, pltpu.roll(x, cols - 1, 1))

    def west_of(x, h):
        return jnp.where(west_edge, h, pltpu.roll(x, 1, 1))

    def north_of(x, h):
        return jnp.where(north_edge, h, pltpu.roll(x, rows - 1, 0))

    def south_of(x, h):
        return jnp.where(south_edge, h, pltpu.roll(x, 1, 0))

    lane_tile = hw_ref.shape[1]

    def column_of(ref, p, at):
        packed = ref[...]
        shift = (at - p) % lane_tile
        if shift:
            packed = pltpu.roll(packed, shift, 1)
        return jnp.concatenate([packed] * (cols // lane_tile), 1)

    def east_halo(p):
        return column_of(he_ref, p, lane_tile - 1)

    def west_halo(p):
        return column_of(hw_ref, p, 0)

    odd = lax.axis_index("lat") % 2 == 1

    def north_halo(p):
        return jnp.where(odd, first_ref[p : p + 1, :], second_ref[p : p + 1, :])

    def south_halo(p):
        return jnp.where(odd, second_ref[p : p + 1, :], first_ref[p : p + 1, :])

    depth_plane = 2 * layer_total
    depth = (wi_ref[...] * sb_ref[...]).astype(jnp.float32)
    dsh[0] = depth
    dsh[1] = east_of(depth, east_halo(depth_plane))
    dsh[2] = west_of(depth, west_halo(depth_plane))
    dsh[3] = north_of(depth, north_halo(depth_plane))
    dsh[4] = south_of(depth, south_halo(depth_plane))

    for k in range(layer_total):
        for src, dst, base in ((t_ref, tsh, 0), (s_ref, ssh, layer_total)):
            x = src[k]
            dst[0, k] = east_of(x, east_halo(base + k))
            dst[1, k] = west_of(x, west_halo(base + k))
            dst[2, k] = north_of(x, north_halo(base + k))
            dst[3, k] = south_of(x, south_halo(base + k))
        x = u_ref[k]
        ush[0, k] = east_of(x, east_halo(depth_plane + 1 + k))
        ush[1, k] = west_of(x, west_halo(depth_plane + 1 + k))
        x = v_ref[k]
        vsh[0, k] = north_of(x, north_halo(depth_plane + 1 + k))
        vsh[1, k] = south_of(x, south_halo(depth_plane + 1 + k))

    def planes(k):
        at = jnp.clip(k, 0, layer_total - 1)
        temp = [t_ref[at]] + [tsh[i, at] for i in range(4)]
        salt = [s_ref[at]] + [ssh[i, at] for i in range(4)]
        rho = [HALINE * sv - THERMAL * tv for tv, sv in zip(temp, salt)]
        return temp, salt, rho

    def wet_at(k):
        inside = jnp.logical_and(k >= 0, k < layer_total)
        level = k.astype(jnp.float32)
        return [
            jnp.where(jnp.logical_and(inside, level < dsh[i]), 1.0, 0.0) for i in range(5)
        ]

    sub_tile = 8

    def whole(x):
        return x

    def west_part(x):
        return x[:, :lane_tile]

    def south_part(x):
        return x[:sub_tile, :]

    def horizontal(fields, kcs, wet, a, b, speed_a, speed_b, part):
        face = part(wet[a]) * part(wet[b])
        temp, salt, rho = fields
        k_temp, k_salt, k_rho = kcs
        slope = jnp.clip(
            -((part(rho[b]) - part(rho[a])) * face)
            / jnp.maximum(0.5 * (k_rho[a] + k_rho[b]), DENSITY_FLOOR),
            -SLOPE_LIMIT,
            SLOPE_LIMIT,
        )
        flow = 0.5 * (part(speed_a) + part(speed_b)) * face
        up, down = jnp.maximum(flow, 0.0), jnp.minimum(flow, 0.0)
        out = []
        for x, kx in ((temp, k_temp), (salt, k_salt)):
            xa, xb = part(x[a]), part(x[b])
            grad = (xb - xa) * face
            out.append(
                up * xa + down * xb
                - DIFFUSIVITY * face * (grad + slope * (0.5 * (kx[a] + kx[b])))
            )
        return out

    def cell_means(x, wet):
        east_grad = (x[1] - x[0]) * (wet[0] * wet[1])
        west_grad = (x[0] - x[2]) * (wet[2] * wet[0])
        north_grad = (x[3] - x[0]) * (wet[0] * wet[3])
        south_grad = (x[0] - x[4]) * (wet[4] * wet[0])
        return 0.5 * (west_grad + east_grad), 0.5 * (south_grad + north_grad)

    def vertical_mean(lo, h, up, face_top, face_bottom, i, part):
        return 0.5 * (
            (part(h[i]) - part(lo[i])) * part(face_top[i])
            + (part(up[i]) - part(h[i])) * part(face_bottom[i])
        )

    def level_step(k, carry):
        down_temp, down_salt = carry[:2]
        means_here = [carry[2 + 2 * n : 4 + 2 * n] for n in range(3)]
        face_top = list(carry[8:13])
        lower = planes(k - 1)
        here = planes(k)
        upper = planes(k + 1)
        wet_here = wet_at(k)
        wet_upper = wet_at(k + 1)
        face_bottom = [wet_upper[i] * wet_here[i] for i in range(5)]

        def kc_set(i, part):
            return [
                vertical_mean(lo, h, up, face_top, face_bottom, i, part)
                for lo, h, up in zip(lower, here, upper)
            ]

        kc_full = [kc_set(i, whole) for i in (0, 1, 3)]
        kcs = [[kc_full[0][n], kc_full[1][n], None, kc_full[2][n], None] for n in range(3)]
        west_kc = kc_set(2, west_part)
        south_kc = kc_set(4, south_part)
        west_kcs = [
            [west_part(kc_full[0][n]), None, west_kc[n], None, None] for n in range(3)
        ]
        south_kcs = [
            [south_part(kc_full[0][n]), None, None, None, south_kc[n]] for n in range(3)
        ]
        zonal = u_ref[k]
        meridional = v_ref[k]
        east = horizontal(here, kcs, wet_here, 0, 1, zonal, ush[0, k], whole)
        west_edge_flux = horizontal(here, west_kcs, wet_here, 2, 0, ush[1, k], zonal, west_part)
        north = horizontal(here, kcs, wet_here, 0, 3, meridional, vsh[0, k], whole)
        south_edge_flux = horizontal(
            here, south_kcs, wet_here, 4, 0, vsh[1, k], meridional, south_part
        )
        west = [
            jnp.where(
                west_edge,
                jnp.concatenate([w] * (cols // lane_tile), 1),
                pltpu.roll(f, 1, 1),
            )
            for w, f in zip(west_edge_flux, east)
        ]
        south = [
            jnp.where(
                south_edge,
                jnp.concatenate([s] * (rows // sub_tile), 0),
                pltpu.roll(f, 1, 0),
            )
            for s, f in zip(south_edge_flux, north)
        ]
        means_upper = [cell_means(f, wet_upper) for f in upper]
        face = face_bottom[0]
        xu = [0.5 * (mh[0] + mu[0]) for mh, mu in zip(means_here, means_upper)]
        yu = [0.5 * (mh[1] + mu[1]) for mh, mu in zip(means_here, means_upper)]
        dk = [(up[0] - h[0]) * face for h, up in zip(here, upper)]
        floor = jnp.maximum(dk[2], DENSITY_FLOOR)
        slope_x = jnp.clip(-xu[2] / floor, -SLOPE_LIMIT, SLOPE_LIMIT)
        slope_y = jnp.clip(-yu[2] / floor, -SLOPE_LIMIT, SLOPE_LIMIT)
        above = jnp.clip(k + 1, 0, layer_total - 1)
        flow = 0.5 * (w_ref[k] + w_ref[above]) * face
        up, down = jnp.maximum(flow, 0.0), jnp.minimum(flow, 0.0)
        squares = slope_x * slope_x + slope_y * slope_y
        below = []
        for n in range(2):
            below.append(
                up * here[n][0] + down * upper[n][0]
                - DIFFUSIVITY * face * (slope_x * xu[n] + slope_y * yu[n] + squares * dk[n])
            )
        for n, (dst, top) in enumerate(((ot_ref, down_temp), (os_ref, down_salt))):
            divergence = (east[n] - west[n]) + (north[n] - south[n])
            divergence = divergence + (below[n] - top)
            dst[k] = here[n][0] - divergence
        return (
            tuple(below) + tuple(m for pair in means_upper for m in pair) + tuple(face_bottom)
        )

    zero = jnp.zeros((rows, cols), jnp.float32)
    first_wet = wet_at(jnp.int32(0))
    first_means = [cell_means(f, first_wet) for f in planes(jnp.int32(0))]
    lax.fori_loop(
        0,
        layer_total,
        level_step,
        (zero, zero) + tuple(m for pair in first_means for m in pair) + (zero,) * 5,
    )


def edge_kernel(
    t_ref, s_ref, u_ref, v_ref, wi_ref, sb_ref,
    west_ref, east_ref, first_ref, second_ref, tops_ref, bottoms_ref,
):
    layer_total, rows, cols = t_ref.shape
    lane_tile = west_ref.shape[1]
    lat_index = lax.axis_index("lat")
    odd = lat_index % 2 == 1
    top = lat_index == lax.axis_size("lat") - 1
    depth = (wi_ref[...] * sb_ref[...]).astype(jnp.float32)
    lane = lax.broadcasted_iota(jnp.int32, (rows, lane_tile), 1)
    column_planes = (
        [t_ref[k] for k in range(layer_total)]
        + [s_ref[k] for k in range(layer_total)]
        + [depth]
        + [u_ref[k] for k in range(layer_total)]
    )
    west = jnp.zeros((rows, lane_tile), jnp.float32)
    east = jnp.zeros((rows, lane_tile), jnp.float32)
    for p, x in enumerate(column_planes):
        west = jnp.where(lane == p, x[:, cols - 1 :], west)
        east = jnp.where(lane == p, x[:, :1], east)
    west_ref[...] = west
    east_ref[...] = east
    base_planes = 2 * layer_total + 1
    row_planes = column_planes[:base_planes] + [v_ref[k] for k in range(layer_total)]
    for p, x in enumerate(row_planes):
        tops_ref[p : p + 1, :] = x[rows - 1 :, :]
        bottoms_ref[p : p + 1, :] = x[:1, :]
    tops = tops_ref[...]
    bottoms = bottoms_ref[...]
    line_lane = lax.broadcasted_iota(jnp.int32, tops.shape, 1)
    mirrored = tops
    step = 1
    while step < cols:
        mirrored = jnp.where(
            (line_lane & step) != 0,
            pltpu.roll(mirrored, step, 1),
            pltpu.roll(mirrored, cols - step, 1),
        )
        step *= 2
    plane = lax.broadcasted_iota(jnp.int32, tops.shape, 0)
    folded = jnp.where(plane >= base_planes, -mirrored, mirrored)
    first_ref[...] = jnp.where(top, folded, jnp.where(odd, tops, bottoms))
    second_ref[...] = jnp.where(odd, bottoms, tops)


def on_device(
    potential_warmth,
    saltiness_anomaly,
    zonal_speed,
    meridional_speed,
    sinking_speed,
    water_indicator,
    seabed_layer_index,
):
    layer_total, rows, cols = potential_warmth.shape
    base_planes = 2 * layer_total + 1
    halo_planes = 3 * layer_total + 1
    lane_tile = 128
    lon_count = lax.axis_size("lon")
    lat_count = lax.axis_size("lat")
    lat_index = lax.axis_index("lat")
    odd = lat_index % 2
    vmem = pltpu.MemorySpace.VMEM
    smem = pltpu.MemorySpace.SMEM
    packed = jax.ShapeDtypeStruct((rows, lane_tile), jnp.float32)
    lines = jax.ShapeDtypeStruct((halo_planes, cols), jnp.float32)
    west_pack, east_pack, first_lines, second_lines = pl.pallas_call(
        edge_kernel,
        out_shape=(packed, packed, lines, lines),
        in_specs=[pl.BlockSpec(memory_space=vmem)] * 6,
        out_specs=tuple(pl.BlockSpec(memory_space=vmem) for _ in range(4)),
        scratch_shapes=[
            pltpu.VMEM((halo_planes, cols), jnp.float32),
            pltpu.VMEM((halo_planes, cols), jnp.float32),
        ],
    )(
        potential_warmth,
        saltiness_anomaly,
        zonal_speed,
        meridional_speed,
        water_indicator,
        seabed_layer_index,
    )

    west_cols = lax.ppermute(
        west_pack, "lon", [(i, (i + 1) % lon_count) for i in range(lon_count)]
    )
    east_cols = lax.ppermute(
        east_pack, "lon", [((i + 1) % lon_count, i) for i in range(lon_count)]
    )

    def device(lat, lon):
        return lon * lat_count + lat

    first_pairs = []
    second_pairs = []
    for lon in range(lon_count):
        for lat in range(lat_count - 1):
            pairs = first_pairs if lat % 2 else second_pairs
            pairs.append((device(lat, lon), device(lat + 1, lon)))
            pairs.append((device(lat + 1, lon), device(lat, lon)))
        first_pairs.append(
            (device(lat_count - 1, lon), device(lat_count - 1, lon_count - 1 - lon))
        )
    first_got = lax.ppermute(first_lines, ("lon", "lat"), first_pairs)
    second_got = lax.ppermute(second_lines, ("lon", "lat"), second_pairs)
    field = jax.ShapeDtypeStruct(potential_warmth.shape, jnp.float32)
    return pl.pallas_call(
        stencil_kernel,
        out_shape=(field, field),
        in_specs=[pl.BlockSpec(memory_space=vmem)] * 11,
        out_specs=(pl.BlockSpec(memory_space=vmem), pl.BlockSpec(memory_space=vmem)),
        scratch_shapes=[
            pltpu.VMEM((4, layer_total, rows, cols), jnp.float32),
            pltpu.VMEM((4, layer_total, rows, cols), jnp.float32),
            pltpu.VMEM((2, layer_total, rows, cols), jnp.float32),
            pltpu.VMEM((2, layer_total, rows, cols), jnp.float32),
            pltpu.VMEM((5, rows, cols), jnp.float32),
        ],
    )(
        potential_warmth,
        saltiness_anomaly,
        zonal_speed,
        meridional_speed,
        sinking_speed,
        water_indicator,
        seabed_layer_index,
        west_cols,
        east_cols,
        first_got,
        second_got,
    )


def solution(mesh):
    placed = (
        P(None, "lat", "lon"),
        P(None, "lat", "lon"),
        P(None, "lat", "lon"),
        P(None, "lat", "lon"),
        P(None, "lat", "lon"),
        P("lat", "lon"),
        P("lat", "lon"),
    )
    return jax.shard_map(
        on_device,
        mesh=mesh,
        in_specs=placed,
        out_specs=(P(None, "lat", "lon"), P(None, "lat", "lon")),
        check_vma=False,
    )
```

```python
import jax
import jax.numpy as jnp
from jax import lax
from jax.experimental import pallas as pl
from jax.experimental.pallas import tpu as pltpu
from jax.sharding import PartitionSpec as P

DIFFUSIVITY = 0.15
DENSITY_FLOOR = 0.5
SLOPE_LIMIT = 1.0
THERMAL = 0.25
HALINE = 0.75


def stencil_kernel(
    t_ref, s_ref, u_ref, v_ref, w_ref, wi_ref, sb_ref, hw_ref, he_ref,
    first_ref, second_ref, ot_ref, os_ref, tsh, ssh, ush, vsh, dsh,
):
    layer_total, rows, cols = t_ref.shape
    lane = lax.broadcasted_iota(jnp.int32, (rows, cols), 1)
    row = lax.broadcasted_iota(jnp.int32, (rows, cols), 0)
    east_edge = lane == cols - 1
    west_edge = lane == 0
    north_edge = row == rows - 1
    south_edge = row == 0

    def east_of(x, h):
        return jnp.where(east_edge, h, pltpu.roll(x, cols - 1, 1))

    def west_of(x, h):
        return jnp.where(west_edge, h, pltpu.roll(x, 1, 1))

    def north_of(x, h):
        return jnp.where(north_edge, h, pltpu.roll(x, rows - 1, 0))

    def south_of(x, h):
        return jnp.where(south_edge, h, pltpu.roll(x, 1, 0))

    lane_tile = hw_ref.shape[1]

    def column_of(ref, p, at):
        packed = ref[...]
        shift = (at - p) % lane_tile
        if shift:
            packed = pltpu.roll(packed, shift, 1)
        return jnp.concatenate([packed] * (cols // lane_tile), 1)

    def east_halo(p):
        return column_of(he_ref, p, lane_tile - 1)

    def west_halo(p):
        return column_of(hw_ref, p, 0)

    odd = lax.axis_index("lat") % 2 == 1

    def north_halo(p):
        return jnp.where(odd, first_ref[p : p + 1, :], second_ref[p : p + 1, :])

    def south_halo(p):
        return jnp.where(odd, second_ref[p : p + 1, :], first_ref[p : p + 1, :])

    depth_plane = 2 * layer_total
    depth = (wi_ref[...] * sb_ref[...]).astype(jnp.float32)
    dsh[0] = depth
    dsh[1] = east_of(depth, east_halo(depth_plane))
    dsh[2] = west_of(depth, west_halo(depth_plane))
    dsh[3] = north_of(depth, north_halo(depth_plane))
    dsh[4] = south_of(depth, south_halo(depth_plane))

    for k in range(layer_total):
        for src, dst, base in ((t_ref, tsh, 0), (s_ref, ssh, layer_total)):
            x = src[k]
            dst[0, k] = east_of(x, east_halo(base + k))
            dst[1, k] = west_of(x, west_halo(base + k))
            dst[2, k] = north_of(x, north_halo(base + k))
            dst[3, k] = south_of(x, south_halo(base + k))
        x = u_ref[k]
        ush[0, k] = east_of(x, east_halo(depth_plane + 1 + k))
        ush[1, k] = west_of(x, west_halo(depth_plane + 1 + k))
        x = v_ref[k]
        vsh[0, k] = north_of(x, north_halo(depth_plane + 1 + k))
        vsh[1, k] = south_of(x, south_halo(depth_plane + 1 + k))

    def planes(k):
        at = jnp.clip(k, 0, layer_total - 1)
        temp = [t_ref[at]] + [tsh[i, at] for i in range(4)]
        salt = [s_ref[at]] + [ssh[i, at] for i in range(4)]
        rho = [HALINE * sv - THERMAL * tv for tv, sv in zip(temp, salt)]
        return temp, salt, rho

    def wet_at(k):
        inside = jnp.logical_and(k >= 0, k < layer_total)
        level = k.astype(jnp.float32)
        return [
            jnp.where(jnp.logical_and(inside, level < dsh[i]), 1.0, 0.0) for i in range(5)
        ]

    sub_tile = 8

    def whole(x):
        return x

    def west_part(x):
        return x[:, :lane_tile]

    def south_part(x):
        return x[:sub_tile, :]

    def horizontal(fields, kcs, wet, a, b, speed_a, speed_b, part):
        face = part(wet[a]) * part(wet[b])
        temp, salt, rho = fields
        k_temp, k_salt, k_rho = kcs
        slope = jnp.clip(
            -((part(rho[b]) - part(rho[a])) * face)
            / jnp.maximum(0.5 * (k_rho[a] + k_rho[b]), DENSITY_FLOOR),
            -SLOPE_LIMIT,
            SLOPE_LIMIT,
        )
        flow = 0.5 * (part(speed_a) + part(speed_b)) * face
        up, down = jnp.maximum(flow, 0.0), jnp.minimum(flow, 0.0)
        out = []
        for x, kx in ((temp, k_temp), (salt, k_salt)):
            xa, xb = part(x[a]), part(x[b])
            grad = (xb - xa) * face
            out.append(
                up * xa + down * xb
                - DIFFUSIVITY * face * (grad + slope * (0.5 * (kx[a] + kx[b])))
            )
        return out

    def cell_means(x, wet):
        east_grad = (x[1] - x[0]) * (wet[0] * wet[1])
        west_grad = (x[0] - x[2]) * (wet[2] * wet[0])
        north_grad = (x[3] - x[0]) * (wet[0] * wet[3])
        south_grad = (x[0] - x[4]) * (wet[4] * wet[0])
        return 0.5 * (west_grad + east_grad), 0.5 * (south_grad + north_grad)

    def vertical_mean(lo, h, up, face_top, face_bottom, i, part):
        return 0.5 * (
            (part(h[i]) - part(lo[i])) * part(face_top[i])
            + (part(up[i]) - part(h[i])) * part(face_bottom[i])
        )

    def level_step(k, carry):
        down_temp, down_salt = carry[:2]
        means_here = [carry[2 + 2 * n : 4 + 2 * n] for n in range(3)]
        face_top = list(carry[8:13])
        lower = planes(k - 1)
        here = planes(k)
        upper = planes(k + 1)
        wet_here = wet_at(k)
        wet_upper = wet_at(k + 1)
        face_bottom = [wet_upper[i] * wet_here[i] for i in range(5)]

        def kc_set(i, part):
            return [
                vertical_mean(lo, h, up, face_top, face_bottom, i, part)
                for lo, h, up in zip(lower, here, upper)
            ]

        kc_full = [kc_set(i, whole) for i in (0, 1, 3)]
        kcs = [[kc_full[0][n], kc_full[1][n], None, kc_full[2][n], None] for n in range(3)]
        west_kcs = [[kc_set(0, west_part)[n], None, kc_set(2, west_part)[n], None, None] for n in range(3)]
        south_kcs = [[kc_set(0, south_part)[n], None, None, None, kc_set(4, south_part)[n]] for n in range(3)]
        zonal = u_ref[k]
        meridional = v_ref[k]
        east = horizontal(here, kcs, wet_here, 0, 1, zonal, ush[0, k], whole)
        west_edge_flux = horizontal(here, west_kcs, wet_here, 2, 0, ush[1, k], zonal, west_part)
        north = horizontal(here, kcs, wet_here, 0, 3, meridional, vsh[0, k], whole)
        south_edge_flux = horizontal(
            here, south_kcs, wet_here, 4, 0, vsh[1, k], meridional, south_part
        )
        west = [
            jnp.where(
                west_edge,
                jnp.concatenate([w] * (cols // lane_tile), 1),
                pltpu.roll(f, 1, 1),
            )
            for w, f in zip(west_edge_flux, east)
        ]
        south = [
            jnp.where(
                south_edge,
                jnp.concatenate([s] * (rows // sub_tile), 0),
                pltpu.roll(f, 1, 0),
            )
            for s, f in zip(south_edge_flux, north)
        ]
        means_upper = [cell_means(f, wet_upper) for f in upper]
        face = face_bottom[0]
        xu = [0.5 * (mh[0] + mu[0]) for mh, mu in zip(means_here, means_upper)]
        yu = [0.5 * (mh[1] + mu[1]) for mh, mu in zip(means_here, means_upper)]
        dk = [(up[0] - h[0]) * face for h, up in zip(here, upper)]
        floor = jnp.maximum(dk[2], DENSITY_FLOOR)
        slope_x = jnp.clip(-xu[2] / floor, -SLOPE_LIMIT, SLOPE_LIMIT)
        slope_y = jnp.clip(-yu[2] / floor, -SLOPE_LIMIT, SLOPE_LIMIT)
        above = jnp.clip(k + 1, 0, layer_total - 1)
        flow = 0.5 * (w_ref[k] + w_ref[above]) * face
        up, down = jnp.maximum(flow, 0.0), jnp.minimum(flow, 0.0)
        squares = slope_x * slope_x + slope_y * slope_y
        below = []
        for n in range(2):
            below.append(
                up * here[n][0] + down * upper[n][0]
                - DIFFUSIVITY * face * (slope_x * xu[n] + slope_y * yu[n] + squares * dk[n])
            )
        for n, (dst, top) in enumerate(((ot_ref, down_temp), (os_ref, down_salt))):
            divergence = (east[n] - west[n]) + (north[n] - south[n])
            divergence = divergence + (below[n] - top)
            dst[k] = here[n][0] - divergence
        return (
            tuple(below) + tuple(m for pair in means_upper for m in pair) + tuple(face_bottom)
        )

    zero = jnp.zeros((rows, cols), jnp.float32)
    first_wet = wet_at(jnp.int32(0))
    first_means = [cell_means(f, first_wet) for f in planes(jnp.int32(0))]
    lax.fori_loop(
        0,
        layer_total,
        level_step,
        (zero, zero) + tuple(m for pair in first_means for m in pair) + (zero,) * 5,
    )


def edge_kernel(
    t_ref, s_ref, u_ref, v_ref, wi_ref, sb_ref,
    west_ref, east_ref, first_ref, second_ref, tops_ref, bottoms_ref,
):
    layer_total, rows, cols = t_ref.shape
    lane_tile = west_ref.shape[1]
    lat_index = lax.axis_index("lat")
    odd = lat_index % 2 == 1
    top = lat_index == lax.axis_size("lat") - 1
    depth = (wi_ref[...] * sb_ref[...]).astype(jnp.float32)
    lane = lax.broadcasted_iota(jnp.int32, (rows, lane_tile), 1)
    column_planes = (
        [t_ref[k] for k in range(layer_total)]
        + [s_ref[k] for k in range(layer_total)]
        + [depth]
        + [u_ref[k] for k in range(layer_total)]
    )
    west = jnp.zeros((rows, lane_tile), jnp.float32)
    east = jnp.zeros((rows, lane_tile), jnp.float32)
    for p, x in enumerate(column_planes):
        last = x[:, cols - lane_tile :]
        first = x[:, :lane_tile]
        if (p + 1) % lane_tile:
            last = pltpu.roll(last, (p + 1) % lane_tile, 1)
        if p % lane_tile:
            first = pltpu.roll(first, p % lane_tile, 1)
        west = jnp.where(lane == p, last, west)
        east = jnp.where(lane == p, first, east)
    west_ref[...] = west
    east_ref[...] = east
    base_planes = 2 * layer_total + 1
    row_planes = column_planes[:base_planes] + [v_ref[k] for k in range(layer_total)]
    for p, x in enumerate(row_planes):
        tops_ref[p : p + 1, :] = x[rows - 1 :, :]
        bottoms_ref[p : p + 1, :] = x[:1, :]
    tops = tops_ref[...]
    bottoms = bottoms_ref[...]
    line_lane = lax.broadcasted_iota(jnp.int32, tops.shape, 1)
    mirrored = tops
    step = 1
    while step < cols:
        mirrored = jnp.where(
            (line_lane & step) != 0,
            pltpu.roll(mirrored, step, 1),
            pltpu.roll(mirrored, cols - step, 1),
        )
        step *= 2
    plane = lax.broadcasted_iota(jnp.int32, tops.shape, 0)
    folded = jnp.where(plane >= base_planes, -mirrored, mirrored)
    first_ref[...] = jnp.where(top, folded, jnp.where(odd, tops, bottoms))
    second_ref[...] = jnp.where(odd, bottoms, tops)


def on_device(
    potential_warmth,
    saltiness_anomaly,
    zonal_speed,
    meridional_speed,
    sinking_speed,
    water_indicator,
    seabed_layer_index,
):
    layer_total, rows, cols = potential_warmth.shape
    base_planes = 2 * layer_total + 1
    halo_planes = 3 * layer_total + 1
    lane_tile = 128
    lon_count = lax.axis_size("lon")
    lat_count = lax.axis_size("lat")
    lat_index = lax.axis_index("lat")
    odd = lat_index % 2
    vmem = pltpu.MemorySpace.VMEM
    smem = pltpu.MemorySpace.SMEM
    packed = jax.ShapeDtypeStruct((rows, lane_tile), jnp.float32)
    lines = jax.ShapeDtypeStruct((halo_planes, cols), jnp.float32)
    west_pack, east_pack, first_lines, second_lines = pl.pallas_call(
        edge_kernel,
        out_shape=(packed, packed, lines, lines),
        in_specs=[pl.BlockSpec(memory_space=vmem)] * 6,
        out_specs=tuple(pl.BlockSpec(memory_space=vmem) for _ in range(4)),
        scratch_shapes=[
            pltpu.VMEM((halo_planes, cols), jnp.float32),
            pltpu.VMEM((halo_planes, cols), jnp.float32),
        ],
    )(
        potential_warmth,
        saltiness_anomaly,
        zonal_speed,
        meridional_speed,
        water_indicator,
        seabed_layer_index,
    )

    west_cols = lax.ppermute(
        west_pack, "lon", [(i, (i + 1) % lon_count) for i in range(lon_count)]
    )
    east_cols = lax.ppermute(
        east_pack, "lon", [((i + 1) % lon_count, i) for i in range(lon_count)]
    )

    def device(lat, lon):
        return lon * lat_count + lat

    first_pairs = []
    second_pairs = []
    for lon in range(lon_count):
        for lat in range(lat_count - 1):
            pairs = first_pairs if lat % 2 else second_pairs
            pairs.append((device(lat, lon), device(lat + 1, lon)))
            pairs.append((device(lat + 1, lon), device(lat, lon)))
        first_pairs.append(
            (device(lat_count - 1, lon), device(lat_count - 1, lon_count - 1 - lon))
        )
    first_got = lax.ppermute(first_lines, ("lon", "lat"), first_pairs)
    second_got = lax.ppermute(second_lines, ("lon", "lat"), second_pairs)
    field = jax.ShapeDtypeStruct(potential_warmth.shape, jnp.float32)
    return pl.pallas_call(
        stencil_kernel,
        out_shape=(field, field),
        in_specs=[pl.BlockSpec(memory_space=vmem)] * 11,
        out_specs=(pl.BlockSpec(memory_space=vmem), pl.BlockSpec(memory_space=vmem)),
        scratch_shapes=[
            pltpu.VMEM((4, layer_total, rows, cols), jnp.float32),
            pltpu.VMEM((4, layer_total, rows, cols), jnp.float32),
            pltpu.VMEM((2, layer_total, rows, cols), jnp.float32),
            pltpu.VMEM((2, layer_total, rows, cols), jnp.float32),
            pltpu.VMEM((5, rows, cols), jnp.float32),
        ],
    )(
        potential_warmth,
        saltiness_anomaly,
        zonal_speed,
        meridional_speed,
        sinking_speed,
        water_indicator,
        seabed_layer_index,
        west_cols,
        east_cols,
        first_got,
        second_got,
    )


def solution(mesh):
    placed = (
        P(None, "lat", "lon"),
        P(None, "lat", "lon"),
        P(None, "lat", "lon"),
        P(None, "lat", "lon"),
        P(None, "lat", "lon"),
        P("lat", "lon"),
        P("lat", "lon"),
    )
    return jax.shard_map(
        on_device,
        mesh=mesh,
        in_specs=placed,
        out_specs=(P(None, "lat", "lon"), P(None, "lat", "lon")),
        check_vma=False,
    )
```
